128 devices in a mesh: seq: 32 (over z, x, core), store: 4 (over y).
Axes of the slice: x: 4, y: 4, z: 4, core: 2. Of those that a mesh axis runs over, the one named last changes fastest.
Arguments:
- queries: bfloat16 [4, 4096, 4096], P('store', 'seq'), may hold values from -12 to 12
- keys: bfloat16 [4, 4096, 512], P('store', 'seq'), may hold values from -6 to 6
- values: bfloat16 [4, 4096, 512], P('store', 'seq'), may hold values from -6 to 6
- segment_ids: int32 [4, 4096], P('store', 'seq'), may hold values from 0 to 3, never falling along the last dimension, each value on 1 to 2048 neighbouring positions
- route_ids: int32 [4, 4096], P('store', 'seq'), may hold values from 0 to 2047, as said below
- adapter_down: bfloat16 [4096, 131072], P(None, ('seq', 'store')), may hold values from -0.09375 to 0.09375
- adapter_up: bfloat16 [131072, 4096], P(('seq', 'store')), may hold values from -0.75 to 0.75
Outputs:
- mixed: bfloat16 [4, 4096, 4096], P('store', 'seq')
The draws below stay inside these ranges and needn't reach their ends.
Inputs may be any that keep to these rules, and one draw needn't show every extreme that they name: `route_ids`: among the 128 tokens of one device (positions j * 128 to j * 128 + 127 of one sequence), at most 2 name adapters of any one owner, the owner of adapter e being the device of flat index e // 16 over seq then store; in every draw some owner gets exactly 2 tokens from every device.
All inputs are finite; a program needn't handle non-finite values.
Results may differ from the reference program's by a relative error of at most 0.006.
Values may be sent and summed in bfloat16 or wider, within the bound.
No kernel may reach another device: no remote copies, remote signals or barrier semaphores. Data moves between devices by JAX's collectives and lax.ppermute only.
A program may use at most 128 MiB of HBM per device.

```python
import math
import jax
import jax.numpy as jnp
import numpy as np
from jax import lax

HEAD_DIM = 128
HEADS = 32
KV_HEADS = 4
RANK = 64
EXP_DEV = 16
TOK_DEV = 128
WIDTH = 4096
LENGTH = 4096
EXPERTS = 2048
CAP = 2
N_SEQ = 32
N_STORE = 4
DEVICES = 128


def draw_queries(key, part):
    inner = jax.random.fold_in(key, 11)
    field = 2.5 * jnp.clip(jax.random.normal(inner, (N_STORE, LENGTH, HEADS, HEAD_DIM), jnp.float32), -4.8, 4.8)
    return field.reshape(N_STORE, LENGTH, HEADS * HEAD_DIM).astype(jnp.bfloat16)


def draw_keys(key, part):
    inner = jax.random.fold_in(key, 13)
    field = jnp.clip(jax.random.normal(inner, (N_STORE, LENGTH, KV_HEADS, HEAD_DIM), jnp.float32), -6.0, 6.0)
    return field.reshape(N_STORE, LENGTH, KV_HEADS * HEAD_DIM).astype(jnp.bfloat16)


def draw_route_ids(key, part):
    hot_owner = jax.random.randint(jax.random.fold_in(key, 21), (), 0, DEVICES)

    def one_block(block_key):
        first, second, third = jax.random.split(block_key, 3)
        others = jnp.arange((DEVICES - 1) * CAP, dtype=jnp.int32) // CAP
        others = others + (others >= hot_owner).astype(jnp.int32)
        picked = jax.random.permutation(first, others)[:TOK_DEV - CAP]
        owners = jnp.concatenate([jnp.full((CAP,), hot_owner, jnp.int32), picked])
        local = jax.random.randint(second, (TOK_DEV,), 0, EXP_DEV)
        return jax.random.permutation(third, owners * EXP_DEV + local)
    block_keys = jax.random.split(jax.random.fold_in(key, 23), N_STORE * N_SEQ)
    blocks = jax.vmap(one_block)(block_keys)
    return blocks.reshape(N_STORE, LENGTH).astype(jnp.int32)


def levels(key, shape, cuts, smallest, high):
    factor_of = 1.0
    for position, blocks in cuts:
        heights = jax.random.uniform(jax.random.fold_in(jax.random.fold_in(key, 6), position), (blocks,), jnp.float32, smallest / len(cuts), high / len(cuts))
        factor_of = factor_of * jnp.repeat(jnp.exp(heights), shape[position] // blocks).reshape((-1,) + (1,) * (len(shape) - 1 - position))
    return factor_of


def split_up(count, total, bound, lean):
    portions = [(1 << 20) // math.isqrt(rank ** lean) + 1 for rank in range(2, count + 1)]
    rest, given = total - bound - (count - 1), [1] * (count - 1)
    while rest > 0:
        candidates = [i for i in range(count - 1) if given[i] < bound]
        whole, budget = sum([portions[i] for i in candidates]), rest
        for i in candidates:
            addition = min(bound - given[i], max(1, budget * portions[i] // whole), rest)
            given[i] = given[i] + addition
            rest = rest - addition
    return np.array([bound] + given)


def ragged(own_key, amount, total, limit, lean):
    if amount == 2:
        one = jax.random.randint(own_key, (), max(1, total - limit), min(limit, total - 1) + 1)
        return jnp.stack([one, total - one])
    tallies = jnp.asarray(split_up(amount, total, limit, lean), jnp.int32)
    pairs = (amount - 1) // 2
    source_of, sink = tallies[1:1 + 2 * pairs:2], tallies[2:2 + 2 * pairs:2]
    slack = jnp.minimum(source_of - 1, limit - sink)
    passed = jax.random.randint(jax.random.fold_in(own_key, 1), (pairs,), 0, 1 << 20) % (slack + 1)
    tallies = tallies.at[1:1 + 2 * pairs:2].set(source_of - passed).at[2:2 + 2 * pairs:2].set(sink + passed)
    return tallies[jax.random.permutation(jax.random.fold_in(own_key, 2), amount)]


def normal_values(own_key, dims, spread, most, cuts=(), kind=jnp.bfloat16):
    array = spread * jax.random.normal(own_key, dims, jnp.float32)
    if cuts:
        array = array * levels(own_key, dims, cuts, -0.22, 0.18)
    return jnp.clip(array, -most, most).astype(kind)


def setup_inputs(seed: int = 0) -> dict:
    splits = jax.random.split(jax.random.key(seed), 8)
    return {
        "queries": draw_queries(jax.random.fold_in(splits[7], 71), 0),
        "keys": draw_keys(jax.random.fold_in(splits[7], 71), 0),
        "values": normal_values(splits[2], (N_STORE, LENGTH, KV_HEADS * HEAD_DIM), 1.0, 6.0, ((0, 4), (1, 32))),
        "segment_ids": jax.vmap(lambda own: jnp.searchsorted(jnp.cumsum(ragged(own, 4, LENGTH, LENGTH // 2, 0)), jnp.arange(LENGTH), side="right"))(jax.random.split(splits[3], N_STORE)).reshape((N_STORE, LENGTH)).astype(jnp.int32),
        "route_ids": draw_route_ids(jax.random.fold_in(splits[7], 71), 0),
        "adapter_down": normal_values(splits[5], (WIDTH, EXPERTS * RANK), WIDTH ** -0.5, 0.09375, ((1, 128),)),
        "adapter_up": normal_values(splits[6], (EXPERTS * RANK, WIDTH), RANK ** -0.5, 0.75, ((0, 128),)),
    }


def attend_one(queries, keys, values, segments):
    length = queries.shape[0]
    group = HEADS // KV_HEADS
    block = min(512, length)
    q_four = queries.reshape(length, KV_HEADS, group, HEAD_DIM)
    k_float = keys.reshape(length, KV_HEADS, HEAD_DIM).astype(jnp.float32)
    v_float = values.reshape(length, KV_HEADS, HEAD_DIM).astype(jnp.float32)
    key_pos = jnp.arange(length, dtype=jnp.int32)
    scale = HEAD_DIM ** -0.5

    def one_block(index):
        start = (index * block).astype(jnp.int32)
        q_block = lax.dynamic_slice_in_dim(q_four, start, block, 0).astype(jnp.float32)
        seg_block = lax.dynamic_slice_in_dim(segments, start, block, 0)
        scores = jnp.einsum('qkgd,nkd->kgqn', q_block, k_float) * scale
        q_pos = start + jnp.arange(block, dtype=jnp.int32)
        allowed = (key_pos[None, :] <= q_pos[:, None]) & (segments[None, :] == seg_block[:, None])
        scores = jnp.where(allowed[None, None], scores, jnp.float32(-1e30))
        top = jnp.max(scores, axis=-1, keepdims=True)
        expo = jnp.exp(scores - top)
        total = jnp.sum(expo, axis=-1)
        weights = expo.astype(jnp.bfloat16).astype(jnp.float32)
        summed = jnp.einsum('kgqn,nkd->qkgd', weights, v_float)
        out = summed / jnp.transpose(total, (2, 0, 1))[:, :, :, None]
        return out.astype(jnp.bfloat16).reshape(block, HEADS * HEAD_DIM)

    blocks = lax.map(one_block, jnp.arange(length // block, dtype=jnp.int32))
    return blocks.reshape(length, HEADS * HEAD_DIM)


def reference(queries, keys, values, segment_ids, route_ids, adapter_down, adapter_up):
    contexts = []
    for index in range(N_STORE):
        contexts.append(attend_one(queries[index], keys[index], values[index], segment_ids[index]))
    context = jnp.stack(contexts).reshape(-1, WIDTH)
    route = route_ids.reshape(-1)
    down_three = adapter_down.reshape(WIDTH, EXPERTS, RANK)
    up_three = adapter_up.reshape(EXPERTS, RANK, WIDTH)
    rows_block = 64

    def one_rows(index):
        start = (index * rows_block).astype(jnp.int32)
        x_rows = lax.dynamic_slice_in_dim(context, start, rows_block, 0).astype(jnp.float32)
        chosen = lax.dynamic_slice_in_dim(route, start, rows_block, 0)
        down_rows = jnp.take(down_three, chosen, axis=1).astype(jnp.float32)
        low = jnp.einsum('tw,wtr->tr', x_rows, down_rows).astype(jnp.bfloat16)
        up_rows = jnp.take(up_three, chosen, axis=0).astype(jnp.float32)
        delta = jnp.einsum('tr,trw->tw', low.astype(jnp.float32), up_rows).astype(jnp.bfloat16)
        return (x_rows + delta.astype(jnp.float32)).astype(jnp.bfloat16)

    mixed = lax.map(one_rows, jnp.arange(context.shape[0] // rows_block, dtype=jnp.int32))
    return mixed.reshape(N_STORE, LENGTH, WIDTH)
```

```python
import jax
import jax.numpy as jnp
from jax import lax
from jax.sharding import PartitionSpec as P

HEAD_DIM = 128
HEADS = 32
KV_HEADS = 4
RANK = 64
EXP_DEV = 16
MAX_DOC = 2048


def attend(queries, key_rows, value_rows, segments):
    length = queries.shape[0]
    block = min(512, length)
    scale = queries.shape[2] ** (-0.5)
    key_pos = jnp.arange(length, dtype=jnp.int32)
    n_blocks = length // block
    reach = min(n_blocks, (MAX_DOC + block - 1) // block + 1)

    def one_block(start, k_lo, width):
        q_block = lax.dynamic_slice_in_dim(queries, start, block, 0)
        seg_block = lax.dynamic_slice_in_dim(segments, start, block, 0)
        k_rows = lax.dynamic_slice_in_dim(key_rows, k_lo, width, 0)
        v_rows = lax.dynamic_slice_in_dim(value_rows, k_lo, width, 0)
        k_seg = lax.dynamic_slice_in_dim(segments, k_lo, width, 0)
        k_pos = k_lo + jnp.arange(width, dtype=jnp.int32)
        scores = (
            jnp.einsum("qhd,nd->hqn", q_block, k_rows, preferred_element_type=jnp.float32) * scale
        )
        q_pos = start + jnp.arange(block, dtype=jnp.int32)
        allowed = (k_pos[None, :] <= q_pos[:, None]) & (k_seg[None, :] == seg_block[:, None])
        scores = jnp.where(allowed[None], scores, jnp.float32(-1e30))
        top = jnp.max(scores, axis=-1, keepdims=True)
        expo = jnp.exp(scores - top)
        total = jnp.sum(expo, axis=-1)
        summed = jnp.einsum(
            "hqn,nd->qhd", expo.astype(jnp.bfloat16), v_rows, preferred_element_type=jnp.float32
        )
        out = summed / jnp.transpose(total)[:, :, None]
        return out.astype(jnp.bfloat16).reshape(block, -1)

    outs = [one_block(i * block, 0, (i + 1) * block) for i in range(min(reach - 1, n_blocks))]
    if n_blocks >= reach:
        width = reach * block
        rest = lax.map(
            lambda i: one_block(i * block, (i + 1) * block - width, width),
            jnp.arange(reach - 1, n_blocks, dtype=jnp.int32),
        )
        outs.append(rest.reshape((n_blocks - reach + 1) * block, -1))
    return jnp.concatenate(outs, axis=0)


def local(queries, keys, values, segment_ids, route_ids, adapter_down, adapter_up):
    n_seq = lax.axis_size("seq")
    n_store = lax.axis_size("store")
    tok_rows = queries.shape[1]
    width = queries.shape[2]
    length = tok_rows * n_seq
    heads_here = HEADS // n_seq
    q_send = queries.reshape(tok_rows, n_seq, heads_here * HEAD_DIM)
    paired = jnp.concatenate(
        [keys.reshape(tok_rows, KV_HEADS, HEAD_DIM), values.reshape(tok_rows, KV_HEADS, HEAD_DIM)],
        axis=2,
    )
    kv_send = jnp.repeat(paired, n_seq // KV_HEADS, axis=1)
    q_all, kv_all = (
        lax.all_to_all(q_send, "seq", split_axis=1, concat_axis=0, tiled=True),
        lax.all_to_all(kv_send, "seq", split_axis=1, concat_axis=0, tiled=True),
    )
    seg_send = jnp.broadcast_to(segment_ids, (n_seq, tok_rows))
    segments = lax.all_to_all(seg_send, "seq", split_axis=0, concat_axis=0, tiled=True).reshape(
        length
    )
    context = attend(q_all, kv_all[:, 0, :HEAD_DIM], kv_all[:, 0, HEAD_DIM:], segments)
    returned_ctx = lax.all_to_all(
        context.reshape(length, 1, heads_here * HEAD_DIM),
        "seq",
        split_axis=0,
        concat_axis=1,
        tiled=True,
    )
    tok_ctx = returned_ctx.reshape(tok_rows, width)
    devices = n_seq * n_store
    capacity = max(2, 2 * tok_rows // devices)
    chosen = route_ids[0]
    owners = chosen // EXP_DEV
    one_hot = (owners[:, None] == jnp.arange(devices, dtype=jnp.int32)[None, :]).astype(jnp.int32)
    slot_of = jnp.sum(jnp.cumsum(one_hot, axis=0) * one_hot, axis=1) - 1
    placed = owners * capacity + slot_of
    send_rows = jnp.zeros((devices * capacity, width), jnp.bfloat16).at[placed].set(tok_ctx)
    send_tags = (
        jnp.full((devices * capacity,), -1.0, jnp.float32)
        .at[placed]
        .set((chosen % EXP_DEV).astype(jnp.float32))
        .astype(jnp.bfloat16)
    )
    got_rows = lax.all_to_all(
        send_rows.reshape(devices, capacity, width),
        ("seq", "store"),
        split_axis=0,
        concat_axis=0,
        tiled=True,
    )
    flat_rows = got_rows.reshape(-1, width)
    low = jnp.dot(flat_rows, adapter_down, preferred_element_type=jnp.float32)
    lane_owner = (jnp.arange(low.shape[1], dtype=jnp.int32) // RANK).astype(jnp.float32)
    keep_mask = (
        lax.all_to_all(
            send_tags.reshape(devices, capacity),
            ("seq", "store"),
            split_axis=0,
            concat_axis=0,
            tiled=True,
        )
        .reshape(-1, 1)
        .astype(jnp.float32)
        == lane_owner[None, :]
    )
    low = jnp.where(keep_mask, low, 0.0).astype(jnp.bfloat16)
    delta = jnp.dot(low, adapter_up, preferred_element_type=jnp.float32).astype(jnp.bfloat16)
    answer = lax.all_to_all(
        delta.reshape(got_rows.shape), ("seq", "store"), split_axis=0, concat_axis=0, tiled=True
    )
    delta_rows = answer.reshape(devices * capacity, width)[placed]
    mixed = (tok_ctx.astype(jnp.float32) + delta_rows.astype(jnp.float32)).astype(jnp.bfloat16)
    return mixed[None]


def solution(mesh):
    return jax.shard_map(
        local,
        mesh=mesh,
        in_specs=(
            P("store", "seq", None),
            P("store", "seq", None),
            P("store", "seq", None),
            P("store", "seq"),
            P("store", "seq"),
            P(None, ("seq", "store")),
            P(("seq", "store"), None),
        ),
        out_specs=P("store", "seq", None),
        check_vma=False,
    )
```

```python
import jax
import jax.numpy as jnp
from jax import lax
from jax.sharding import PartitionSpec as P

HEAD_DIM = 128
HEADS = 32
KV_HEADS = 4
RANK = 64
EXP_DEV = 16
MAX_DOC = 2048


def attend(queries, key_rows, value_rows, segments):
    length = queries.shape[0]
    block = min(512, length)
    scale = queries.shape[2] ** (-0.5)
    key_pos = jnp.arange(length, dtype=jnp.int32)
    n_blocks = length // block
    reach = min(n_blocks, (MAX_DOC + block - 1) // block + 1)

    def one_block(start, k_lo, width):
        q_block = lax.dynamic_slice_in_dim(queries, start, block, 0)
        seg_block = lax.dynamic_slice_in_dim(segments, start, block, 0)
        k_rows = lax.dynamic_slice_in_dim(key_rows, k_lo, width, 0)
        v_rows = lax.dynamic_slice_in_dim(value_rows, k_lo, width, 0)
        k_seg = lax.dynamic_slice_in_dim(segments, k_lo, width, 0)
        k_pos = k_lo + jnp.arange(width, dtype=jnp.int32)
        scores = (
            jnp.einsum("qhd,nd->hqn", q_block, k_rows, preferred_element_type=jnp.float32) * scale
        )
        q_pos = start + jnp.arange(block, dtype=jnp.int32)
        allowed = (k_pos[None, :] <= q_pos[:, None]) & (k_seg[None, :] == seg_block[:, None])
        scores = jnp.where(allowed[None], scores, jnp.float32(-1e30))
        top = jnp.max(scores, axis=-1, keepdims=True)
        expo = jnp.exp(scores - top)
        total = jnp.sum(expo, axis=-1)
        summed = jnp.einsum(
            "hqn,nd->qhd", expo.astype(jnp.bfloat16), v_rows, preferred_element_type=jnp.float32
        )
        out = summed / jnp.transpose(total)[:, :, None]
        return out.astype(jnp.bfloat16).reshape(block, -1)

    outs = [one_block(i * block, 0, (i + 1) * block) for i in range(min(reach - 1, n_blocks))]
    if n_blocks >= reach:
        width = reach * block
        rest = lax.map(
            lambda i: one_block(i * block, (i + 1) * block - width, width),
            jnp.arange(reach - 1, n_blocks, dtype=jnp.int32),
        )
        outs.append(rest.reshape((n_blocks - reach + 1) * block, -1))
    return jnp.concatenate(outs, axis=0)


def local(queries, keys, values, segment_ids, route_ids, adapter_down, adapter_up):
    n_seq = lax.axis_size("seq")
    n_store = lax.axis_size("store")
    tok_rows = queries.shape[1]
    width = queries.shape[2]
    length = tok_rows * n_seq
    heads_here = HEADS // n_seq
    feat = heads_here * HEAD_DIM
    group = HEADS // KV_HEADS
    devices = n_seq * n_store
    capacity = max(2, 2 * tok_rows // devices)
    slots = n_seq * capacity

    q_send = queries[0].reshape(tok_rows, n_seq, feat)
    paired = jnp.concatenate(
        [keys[0].reshape(tok_rows, KV_HEADS, HEAD_DIM), values[0].reshape(tok_rows, KV_HEADS, HEAD_DIM)],
        axis=2,
    )
    kv_send = jnp.take(paired, (jnp.arange(n_seq) * heads_here) // group, axis=1)
    chosen = route_ids[0]
    meta = jnp.concatenate(
        [segment_ids[0], chosen // EXP_DEV, chosen % EXP_DEV]
    ).astype(jnp.bfloat16)
    meta_w = feat + 2 * HEAD_DIM
    meta = jnp.pad(meta, (0, meta_w - meta.shape[0]))
    payload = jnp.concatenate(
        [
            jnp.concatenate([q_send, kv_send], axis=2),
            jnp.broadcast_to(meta[None, None, :], (1, n_seq, meta_w)),
        ],
        axis=0,
    )
    got_in = lax.all_to_all(payload, "seq", split_axis=1, concat_axis=0, tiled=True)
    got_in = got_in.reshape(n_seq, tok_rows + 1, meta_w)
    q_all = got_in[:, :tok_rows, :feat].reshape(length, heads_here, HEAD_DIM)
    k_all = got_in[:, :tok_rows, feat : feat + HEAD_DIM].reshape(length, HEAD_DIM)
    v_all = got_in[:, :tok_rows, feat + HEAD_DIM :].reshape(length, HEAD_DIM)
    meta_all = got_in[:, tok_rows, : 3 * tok_rows].astype(jnp.int32)
    segments = meta_all[:, :tok_rows].reshape(length)
    owner_all = meta_all[:, tok_rows : 2 * tok_rows]
    adapter_all = meta_all[:, 2 * tok_rows :].reshape(length)

    context = attend(q_all, k_all, v_all, segments).reshape(length, feat)

    def ranks(owner_rows):
        one_hot = (owner_rows[..., None] == jnp.arange(devices, dtype=jnp.int32)).astype(jnp.int32)
        return jnp.sum(jnp.cumsum(one_hot, axis=-2) * one_hot, axis=-1) - 1

    slot_all = (
        jnp.arange(n_seq, dtype=jnp.int32)[:, None] * capacity + ranks(owner_all)
    ).reshape(length)
    target = owner_all.reshape(length) * slots + slot_all
    pick = jnp.full((devices * slots,), length, jnp.int32).at[target].set(
        jnp.arange(length, dtype=jnp.int32)
    )
    tags = jnp.full((devices * slots,), -1, jnp.int32).at[target].set(adapter_all)
    ctx_ext = jnp.concatenate([context, jnp.zeros((1, feat), context.dtype)], axis=0)
    send = ctx_ext[pick].reshape(devices, slots, feat)
    tag_row = jnp.pad(tags.reshape(devices, slots).astype(jnp.bfloat16), ((0, 0), (0, feat - slots)))
    send = jnp.concatenate([send, tag_row[:, None, :]], axis=1)
    got = lax.all_to_all(send, ("seq", "store"), split_axis=0, concat_axis=0, tiled=True)
    got = got.reshape(n_seq, n_store, slots + 1, feat)
    rows = jnp.transpose(got[:, :, :slots, :], (1, 2, 0, 3)).reshape(n_store * slots, width)
    row_tags = got[0, :, slots, :slots].reshape(n_store * slots, 1).astype(jnp.float32)

    low = jnp.dot(rows, adapter_down, preferred_element_type=jnp.float32)
    lane_owner = (jnp.arange(low.shape[1], dtype=jnp.int32) // RANK).astype(jnp.float32)
    low = jnp.where(row_tags == lane_owner[None, :], low, 0.0).astype(jnp.bfloat16)
    delta = jnp.dot(low, adapter_up, preferred_element_type=jnp.float32).astype(jnp.bfloat16)
    mixed_rows = (rows.astype(jnp.float32) + delta.astype(jnp.float32)).astype(jnp.bfloat16)
    ret = jnp.transpose(
        mixed_rows.reshape(n_store, n_seq, capacity, width), (1, 0, 2, 3)
    ).reshape(devices, capacity, width)
    back = lax.all_to_all(ret, ("seq", "store"), split_axis=0, concat_axis=0, tiled=True)
    owners = chosen // EXP_DEV
    placed = owners * capacity + ranks(owners)
    mixed = back.reshape(devices * capacity, width)[placed]
    return mixed[None]


def solution(mesh):
    return jax.shard_map(
        local,
        mesh=mesh,
        in_specs=(
            P("store", "seq", None),
            P("store", "seq", None),
            P("store", "seq", None),
            P("store", "seq"),
            P("store", "seq"),
            P(None, ("seq", "store")),
            P(("seq", "store"), None),
        ),
        out_specs=P("store", "seq", None),
        check_vma=False,
    )
```

```python
import jax
import jax.numpy as jnp
from jax import lax
from jax.sharding import PartitionSpec as P

HEAD_DIM = 128
HEADS = 32
KV_HEADS = 4
RANK = 64
EXP_DEV = 16
MAX_DOC = 2048


def attend(queries, key_rows, value_rows, segments):
    length = queries.shape[0]
    block = min(512, length)
    scale = queries.shape[2] ** (-0.5)
    key_pos = jnp.arange(length, dtype=jnp.int32)
    n_blocks = length // block
    reach = min(n_blocks, (MAX_DOC + block - 1) // block + 1)

    def one_block(start, k_lo, width):
        q_block = lax.dynamic_slice_in_dim(queries, start, block, 0)
        seg_block = lax.dynamic_slice_in_dim(segments, start, block, 0)
        k_rows = lax.dynamic_slice_in_dim(key_rows, k_lo, width, 0)
        v_rows = lax.dynamic_slice_in_dim(value_rows, k_lo, width, 0)
        k_seg = lax.dynamic_slice_in_dim(segments, k_lo, width, 0)
        k_pos = k_lo + jnp.arange(width, dtype=jnp.int32)
        scores = (
            jnp.einsum("qhd,nd->hqn", q_block, k_rows, preferred_element_type=jnp.float32) * scale
        )
        q_pos = start + jnp.arange(block, dtype=jnp.int32)
        allowed = (k_pos[None, :] <= q_pos[:, None]) & (k_seg[None, :] == seg_block[:, None])
        scores = jnp.where(allowed[None], scores, jnp.float32(-1e30))
        top = jnp.max(scores, axis=-1, keepdims=True)
        expo = jnp.exp(scores - top)
        total = jnp.sum(expo, axis=-1)
        summed = jnp.einsum(
            "hqn,nd->qhd", expo.astype(jnp.bfloat16), v_rows, preferred_element_type=jnp.float32
        )
        out = summed / jnp.transpose(total)[:, :, None]
        return out.astype(jnp.bfloat16).reshape(block, -1)

    outs = [one_block(i * block, 0, (i + 1) * block) for i in range(min(reach - 1, n_blocks))]
    if n_blocks >= reach:
        width = reach * block
        rest = lax.map(
            lambda i: one_block(i * block, (i + 1) * block - width, width),
            jnp.arange(reach - 1, n_blocks, dtype=jnp.int32),
        )
        outs.append(rest.reshape((n_blocks - reach + 1) * block, -1))
    return jnp.concatenate(outs, axis=0)


def local(queries, keys, values, segment_ids, route_ids, adapter_down, adapter_up):
    n_seq = lax.axis_size("seq")
    n_store = lax.axis_size("store")
    tok_rows = queries.shape[1]
    width = queries.shape[2]
    length = tok_rows * n_seq
    heads_here = HEADS // n_seq
    feat = heads_here * HEAD_DIM
    group = HEADS // KV_HEADS
    devices = n_seq * n_store
    capacity = max(2, 2 * tok_rows // devices)
    slots = n_seq * capacity

    q_send = queries[0].reshape(tok_rows, n_seq, feat)
    paired = jnp.concatenate(
        [keys[0].reshape(tok_rows, KV_HEADS, HEAD_DIM), values[0].reshape(tok_rows, KV_HEADS, HEAD_DIM)],
        axis=2,
    )
    kv_send = jnp.take(paired, (jnp.arange(n_seq) * heads_here) // group, axis=1)
    chosen = route_ids[0]
    meta = jnp.concatenate(
        [segment_ids[0], chosen // EXP_DEV, chosen % EXP_DEV]
    ).astype(jnp.bfloat16)
    meta_w = feat + 2 * HEAD_DIM
    meta = jnp.pad(meta, (0, meta_w - meta.shape[0]))
    payload = jnp.concatenate(
        [
            jnp.concatenate([q_send, kv_send], axis=2),
            jnp.broadcast_to(meta[None, None, :], (1, n_seq, meta_w)),
        ],
        axis=0,
    )
    got_in = lax.all_to_all(payload, "seq", split_axis=1, concat_axis=0, tiled=True)
    got_in = got_in.reshape(n_seq, tok_rows + 1, meta_w)
    q_all = got_in[:, :tok_rows, :feat].reshape(length, heads_here, HEAD_DIM)
    k_all = got_in[:, :tok_rows, feat : feat + HEAD_DIM].reshape(length, HEAD_DIM)
    v_all = got_in[:, :tok_rows, feat + HEAD_DIM :].reshape(length, HEAD_DIM)
    meta_all = got_in[:, tok_rows, : 3 * tok_rows].astype(jnp.int32)
    segments = meta_all[:, :tok_rows].reshape(length)
    owner_all = meta_all[:, tok_rows : 2 * tok_rows]
    adapter_all = meta_all[:, 2 * tok_rows :]

    context = attend(q_all, k_all, v_all, segments).reshape(length, feat)

    def ranks(owner_rows):
        one_hot = (owner_rows[..., None] == jnp.arange(devices, dtype=jnp.int32)).astype(jnp.int32)
        return jnp.sum(jnp.cumsum(one_hot, axis=-2) * one_hot, axis=-1) - 1

    pick = (
        owner_all * capacity + ranks(owner_all)
    )[:, None, :] == jnp.arange(devices * capacity, dtype=jnp.int32)[None, :, None]
    pick = pick.astype(jnp.bfloat16)
    send = jnp.einsum(
        "jmt,jtf->mjf",
        pick,
        context.reshape(n_seq, tok_rows, feat),
        preferred_element_type=jnp.float32,
    ).astype(jnp.bfloat16)
    send = send.reshape(devices, slots, feat)
    tags = jnp.einsum(
        "jmt,jt->mj",
        pick,
        (adapter_all.reshape(n_seq, tok_rows) + 1).astype(jnp.bfloat16),
        preferred_element_type=jnp.float32,
    ).reshape(devices, slots) - 1.0
    tag_row = jnp.pad(tags.astype(jnp.bfloat16), ((0, 0), (0, feat - slots)))
    send = jnp.concatenate([send, tag_row[:, None, :]], axis=1)
    got = lax.all_to_all(send, ("seq", "store"), split_axis=0, concat_axis=0, tiled=True)
    got = got.reshape(n_seq, n_store, slots + 1, feat)
    rows = jnp.transpose(got[:, :, :slots, :], (1, 2, 0, 3)).reshape(n_store * slots, width)
    row_tags = got[0, :, slots, :slots].reshape(n_store * slots, 1).astype(jnp.float32)

    low = jnp.dot(rows, adapter_down, preferred_element_type=jnp.float32)
    lane_owner = (jnp.arange(low.shape[1], dtype=jnp.int32) // RANK).astype(jnp.float32)
    low = jnp.where(row_tags == lane_owner[None, :], low, 0.0).astype(jnp.bfloat16)
    delta = jnp.dot(low, adapter_up, preferred_element_type=jnp.float32).astype(jnp.bfloat16)
    mixed_rows = (rows.astype(jnp.float32) + delta.astype(jnp.float32)).astype(jnp.bfloat16)
    ret = jnp.transpose(
        mixed_rows.reshape(n_store, capacity, n_seq, width), (2, 0, 1, 3)
    ).reshape(devices, capacity, width)
    back = lax.all_to_all(ret, ("seq", "store"), split_axis=0, concat_axis=0, tiled=True)
    owners = chosen // EXP_DEV
    placed = owners * capacity + ranks(owners)
    mixed = back.reshape(devices * capacity, width)[placed]
    return mixed[None]


def solution(mesh):
    return jax.shard_map(
        local,
        mesh=mesh,
        in_specs=(
            P("store", "seq", None),
            P("store", "seq", None),
            P("store", "seq", None),
            P("store", "seq"),
            P("store", "seq"),
            P(None, ("seq", "store")),
            P(("seq", "store"), None),
        ),
        out_specs=P("store", "seq", None),
        check_vma=False,
    )
```

```python
import functools

import jax
import jax.numpy as jnp
from jax import lax
from jax.experimental import pallas as pl
from jax.experimental.pallas import tpu as pltpu
from jax.sharding import PartitionSpec as P

HEAD_DIM = 128
HEADS = 32
KV_HEADS = 4
RANK = 64
EXP_DEV = 16
MAX_DOC = 2048


def _attn_kernel(lo_ref, q_ref, k_ref, v_ref, qs_ref, o_ref, *, bq, bk, scale):
    i = pl.program_id(0)
    q = q_ref[...]
    qs = qs_ref[...]
    qpos = i * bq + lax.broadcasted_iota(jnp.int32, (bq, 1), 0)
    lo = lo_ref[i]
    hi = (i * bq + bq + bk - 1) // bk

    def scores(kb):
        start = pl.multiple_of(kb * bk, bk)
        k = k_ref[pl.ds(start, bk), :]
        s = lax.dot_general(
            q, k, (((1,), (1,)), ((), ())), preferred_element_type=jnp.float32
        ) * scale
        kpos = start + lax.broadcasted_iota(jnp.int32, (1, bk), 1)
        ok = (kpos >= qs) & (kpos <= qpos)
        return jnp.where(ok, s, jnp.float32(-1e30)), start

    def max_body(kb, m):
        s, _ = scores(kb)
        return jnp.maximum(m, jnp.max(s, axis=1, keepdims=True))

    m = lax.fori_loop(lo, hi, max_body, jnp.full((bq, 1), -1e30, jnp.float32))

    def sum_body(kb, carry):
        total, acc = carry
        s, start = scores(kb)
        p = jnp.exp(s - m)
        total = total + jnp.sum(p, axis=1, keepdims=True)
        v = v_ref[pl.ds(start, bk), :]
        acc = acc + jnp.dot(p.astype(jnp.bfloat16), v, preferred_element_type=jnp.float32)
        return total, acc

    total, acc = lax.fori_loop(
        lo,
        hi,
        sum_body,
        (jnp.zeros((bq, 1), jnp.float32), jnp.zeros((bq, q.shape[1]), jnp.float32)),
    )
    o_ref[...] = (acc / total).astype(o_ref.dtype)


def attend(queries, key_rows, value_rows, segments):
    length, dim = key_rows.shape
    bq = min(256, length)
    bk = min(256, length)
    n_q = length // bq
    pos = jnp.arange(length, dtype=jnp.int32)
    boundary = jnp.concatenate(
        [jnp.ones((1,), jnp.bool_), segments[1:] != segments[:-1]]
    )
    doc_start = lax.cummax(jnp.where(boundary, pos, 0), axis=0)
    lo_blk = doc_start[::bq] // bk
    q_rows = queries.reshape(length, dim)
    kernel = functools.partial(_attn_kernel, bq=bq, bk=bk, scale=dim ** (-0.5))
    out = pl.pallas_call(
        kernel,
        out_shape=jax.ShapeDtypeStruct((length, dim), jnp.bfloat16),
        grid_spec=pltpu.PrefetchScalarGridSpec(
            num_scalar_prefetch=1,
            grid=(n_q,),
            in_specs=[
                pl.BlockSpec((bq, dim), lambda i, lo: (i, 0)),
                pl.BlockSpec((length, dim), lambda i, lo: (0, 0)),
                pl.BlockSpec((length, dim), lambda i, lo: (0, 0)),
                pl.BlockSpec((bq, 1), lambda i, lo: (i, 0)),
            ],
            out_specs=pl.BlockSpec((bq, dim), lambda i, lo: (i, 0)),
        ),
        cost_estimate=pl.CostEstimate(
            flops=6 * length * MAX_DOC * dim,
            transcendentals=length * MAX_DOC,
            bytes_accessed=8 * length * dim,
        ),
    )(lo_blk, q_rows, key_rows, value_rows, doc_start.reshape(length, 1))
    return out


def local(queries, keys, values, segment_ids, route_ids, adapter_down, adapter_up):
    n_seq = lax.axis_size("seq")
    n_store = lax.axis_size("store")
    tok_rows = queries.shape[1]
    width = queries.shape[2]
    length = tok_rows * n_seq
    heads_here = HEADS // n_seq
    feat = heads_here * HEAD_DIM
    group = HEADS // KV_HEADS
    devices = n_seq * n_store
    capacity = max(2, 2 * tok_rows // devices)
    slots = n_seq * capacity

    q_send = queries[0].reshape(tok_rows, n_seq, feat)
    paired = jnp.concatenate(
        [keys[0].reshape(tok_rows, KV_HEADS, HEAD_DIM), values[0].reshape(tok_rows, KV_HEADS, HEAD_DIM)],
        axis=2,
    )
    kv_send = jnp.take(paired, (jnp.arange(n_seq) * heads_here) // group, axis=1)
    chosen = route_ids[0]
    meta = jnp.concatenate(
        [segment_ids[0], chosen // EXP_DEV, chosen % EXP_DEV]
    ).astype(jnp.bfloat16)
    meta_w = feat + 2 * HEAD_DIM
    meta = jnp.pad(meta, (0, meta_w - meta.shape[0]))
    payload = jnp.concatenate(
        [
            jnp.concatenate([q_send, kv_send], axis=2),
            jnp.broadcast_to(meta[None, None, :], (1, n_seq, meta_w)),
        ],
        axis=0,
    )
    got_in = lax.all_to_all(payload, "seq", split_axis=1, concat_axis=0, tiled=True)
    got_in = got_in.reshape(n_seq, tok_rows + 1, meta_w)
    q_all = got_in[:, :tok_rows, :feat].reshape(length, heads_here, HEAD_DIM)
    k_all = got_in[:, :tok_rows, feat : feat + HEAD_DIM].reshape(length, HEAD_DIM)
    v_all = got_in[:, :tok_rows, feat + HEAD_DIM :].reshape(length, HEAD_DIM)
    meta_all = got_in[:, tok_rows, : 3 * tok_rows].astype(jnp.int32)
    segments = meta_all[:, :tok_rows].reshape(length)
    owner_all = meta_all[:, tok_rows : 2 * tok_rows]
    adapter_all = meta_all[:, 2 * tok_rows :]

    context = attend(q_all, k_all, v_all, segments).reshape(length, feat)

    def ranks(owner_rows):
        one_hot = (owner_rows[..., None] == jnp.arange(devices, dtype=jnp.int32)).astype(jnp.int32)
        return jnp.sum(jnp.cumsum(one_hot, axis=-2) * one_hot, axis=-1) - 1

    pick = (
        owner_all * capacity + ranks(owner_all)
    )[:, None, :] == jnp.arange(devices * capacity, dtype=jnp.int32)[None, :, None]
    pick = pick.astype(jnp.bfloat16)
    send = jnp.einsum(
        "jmt,jtf->mjf",
        pick,
        context.reshape(n_seq, tok_rows, feat),
        preferred_element_type=jnp.float32,
    ).astype(jnp.bfloat16)
    send = send.reshape(devices, slots, feat)
    tags = jnp.einsum(
        "jmt,jt->mj",
        pick,
        (adapter_all.reshape(n_seq, tok_rows) + 1).astype(jnp.bfloat16),
        preferred_element_type=jnp.float32,
    ).reshape(devices, slots) - 1.0
    tag_row = jnp.pad(tags.astype(jnp.bfloat16), ((0, 0), (0, feat - slots)))
    send = jnp.concatenate([send, tag_row[:, None, :]], axis=1)
    got = lax.all_to_all(send, ("seq", "store"), split_axis=0, concat_axis=0, tiled=True)
    got = got.reshape(n_seq, n_store, slots + 1, feat)
    rows = jnp.transpose(got[:, :, :slots, :], (1, 2, 0, 3)).reshape(n_store * slots, width)
    row_tags = got[0, :, slots, :slots].reshape(n_store * slots, 1).astype(jnp.float32)

    low = jnp.dot(rows, adapter_down, preferred_element_type=jnp.float32)
    lane_owner = (jnp.arange(low.shape[1], dtype=jnp.int32) // RANK).astype(jnp.float32)
    low = jnp.where(row_tags == lane_owner[None, :], low, 0.0).astype(jnp.bfloat16)
    delta = jnp.dot(low, adapter_up, preferred_element_type=jnp.float32).astype(jnp.bfloat16)
    mixed_rows = (rows.astype(jnp.float32) + delta.astype(jnp.float32)).astype(jnp.bfloat16)
    ret = jnp.transpose(
        mixed_rows.reshape(n_store, capacity, n_seq, width), (2, 0, 1, 3)
    ).reshape(devices, capacity, width)
    back = lax.all_to_all(ret, ("seq", "store"), split_axis=0, concat_axis=0, tiled=True)
    owners = chosen // EXP_DEV
    placed = owners * capacity + ranks(owners)
    mixed = back.reshape(devices * capacity, width)[placed]
    return mixed[None]


def solution(mesh):
    return jax.shard_map(
        local,
        mesh=mesh,
        in_specs=(
            P("store", "seq", None),
            P("store", "seq", None),
            P("store", "seq", None),
            P("store", "seq"),
            P("store", "seq"),
            P(None, ("seq", "store")),
            P(("seq", "store"), None),
        ),
        out_specs=P("store", "seq", None),
        check_vma=False,
    )
```

```python
import functools

import jax
import jax.numpy as jnp
from jax import lax
from jax.experimental import pallas as pl
from jax.experimental.pallas import tpu as pltpu
from jax.sharding import PartitionSpec as P

HEAD_DIM = 128
HEADS = 32
KV_HEADS = 4
RANK = 64
EXP_DEV = 16
MAX_DOC = 2048


def _attn_kernel(lo_ref, full_ref, q_ref, k_ref, v_ref, qs_ref, o_ref, *, bq, bk, scale):
    i = pl.program_id(0)
    lanes = 128
    q = q_ref[...]
    qs = qs_ref[...]
    qpos = i * bq + lax.broadcasted_iota(jnp.int32, (bq, 1), 0)
    lo = lo_ref[i]
    mid = jnp.clip(full_ref[i], lo, i)

    def raw(kb):
        start = pl.multiple_of(kb * bk, bk)
        k = k_ref[pl.ds(start, bk), :]
        s = lax.dot_general(
            q, k, (((1,), (1,)), ((), ())), preferred_element_type=jnp.float32
        ) * scale
        return s, start

    def masked(kb):
        s, start = raw(kb)
        kpos = start + lax.broadcasted_iota(jnp.int32, (1, bk), 1)
        ok = (kpos >= qs) & (kpos <= qpos)
        return jnp.where(ok, s, jnp.float32(-1e30)), start

    def fold_max(m, s):
        for c in range(bk // lanes):
            m = jnp.maximum(m, s[:, c * lanes : (c + 1) * lanes])
        return m

    m = jnp.full((bq, lanes), -1e30, jnp.float32)
    m = lax.fori_loop(lo, mid, lambda kb, m: fold_max(m, masked(kb)[0]), m)
    m = lax.fori_loop(mid, i, lambda kb, m: fold_max(m, raw(kb)[0]), m)
    m = fold_max(m, masked(i)[0])
    top = jnp.max(m, axis=1, keepdims=True)

    def accum(carry, s, start):
        tot, acc = carry
        p = jnp.exp(s - top)
        for c in range(bk // lanes):
            tot = tot + p[:, c * lanes : (c + 1) * lanes]
        v = v_ref[pl.ds(start, bk), :]
        acc = acc + jnp.dot(p.astype(jnp.bfloat16), v, preferred_element_type=jnp.float32)
        return tot, acc

    carry = (jnp.zeros((bq, lanes), jnp.float32), jnp.zeros((bq, q.shape[1]), jnp.float32))
    carry = lax.fori_loop(lo, mid, lambda kb, c: accum(c, *masked(kb)), carry)
    carry = lax.fori_loop(mid, i, lambda kb, c: accum(c, *raw(kb)), carry)
    tot, acc = accum(carry, *masked(i))
    total = jnp.sum(tot, axis=1, keepdims=True)
    o_ref[...] = (acc / total).astype(o_ref.dtype)


def attend(queries, key_rows, value_rows, segments):
    length, dim = key_rows.shape
    bq = min(256, length)
    bk = min(256, length)
    n_q = length // bq
    pos = jnp.arange(length, dtype=jnp.int32)
    boundary = jnp.concatenate(
        [jnp.ones((1,), jnp.bool_), segments[1:] != segments[:-1]]
    )
    doc_start = lax.cummax(jnp.where(boundary, pos, 0), axis=0)
    lo_blk = doc_start[::bq] // bk
    full_blk = (doc_start[bq - 1 :: bq] + bk - 1) // bk
    q_rows = queries.reshape(length, dim)
    kernel = functools.partial(_attn_kernel, bq=bq, bk=bk, scale=dim ** (-0.5))
    out = pl.pallas_call(
        kernel,
        out_shape=jax.ShapeDtypeStruct((length, dim), jnp.bfloat16),
        grid_spec=pltpu.PrefetchScalarGridSpec(
            num_scalar_prefetch=2,
            grid=(n_q,),
            in_specs=[
                pl.BlockSpec((bq, dim), lambda i, lo, full: (i, 0)),
                pl.BlockSpec((length, dim), lambda i, lo, full: (0, 0)),
                pl.BlockSpec((length, dim), lambda i, lo, full: (0, 0)),
                pl.BlockSpec((bq, 1), lambda i, lo, full: (i, 0)),
            ],
            out_specs=pl.BlockSpec((bq, dim), lambda i, lo, full: (i, 0)),
        ),
        cost_estimate=pl.CostEstimate(
            flops=6 * length * MAX_DOC * dim,
            transcendentals=length * MAX_DOC,
            bytes_accessed=8 * length * dim,
        ),
    )(lo_blk, full_blk, q_rows, key_rows, value_rows, doc_start.reshape(length, 1))
    return out


def local(queries, keys, values, segment_ids, route_ids, adapter_down, adapter_up):
    n_seq = lax.axis_size("seq")
    n_store = lax.axis_size("store")
    tok_rows = queries.shape[1]
    width = queries.shape[2]
    length = tok_rows * n_seq
    heads_here = HEADS // n_seq
    feat = heads_here * HEAD_DIM
    group = HEADS // KV_HEADS
    devices = n_seq * n_store
    capacity = max(2, 2 * tok_rows // devices)
    slots = n_seq * capacity

    q_send = queries[0].reshape(tok_rows, n_seq, feat)
    paired = jnp.concatenate(
        [keys[0].reshape(tok_rows, KV_HEADS, HEAD_DIM), values[0].reshape(tok_rows, KV_HEADS, HEAD_DIM)],
        axis=2,
    )
    kv_send = jnp.take(paired, (jnp.arange(n_seq) * heads_here) // group, axis=1)
    chosen = route_ids[0]
    meta = jnp.concatenate(
        [segment_ids[0], chosen // EXP_DEV, chosen % EXP_DEV]
    ).astype(jnp.bfloat16)
    meta_w = feat + 2 * HEAD_DIM
    meta = jnp.pad(meta, (0, meta_w - meta.shape[0]))
    payload = jnp.concatenate(
        [
            jnp.concatenate([q_send, kv_send], axis=2),
            jnp.broadcast_to(meta[None, None, :], (1, n_seq, meta_w)),
        ],
        axis=0,
    )
    got_in = lax.all_to_all(payload, "seq", split_axis=1, concat_axis=0, tiled=True)
    got_in = got_in.reshape(n_seq, tok_rows + 1, meta_w)
    q_all = got_in[:, :tok_rows, :feat].reshape(length, heads_here, HEAD_DIM)
    k_all = got_in[:, :tok_rows, feat : feat + HEAD_DIM].reshape(length, HEAD_DIM)
    v_all = got_in[:, :tok_rows, feat + HEAD_DIM :].reshape(length, HEAD_DIM)
    meta_all = got_in[:, tok_rows, : 3 * tok_rows].astype(jnp.int32)
    segments = meta_all[:, :tok_rows].reshape(length)
    owner_all = meta_all[:, tok_rows : 2 * tok_rows]
    adapter_all = meta_all[:, 2 * tok_rows :]

    context = attend(q_all, k_all, v_all, segments).reshape(length, feat)

    def ranks(owner_rows):
        one_hot = (owner_rows[..., None] == jnp.arange(devices, dtype=jnp.int32)).astype(jnp.int32)
        return jnp.sum(jnp.cumsum(one_hot, axis=-2) * one_hot, axis=-1) - 1

    pick = (
        owner_all * capacity + ranks(owner_all)
    )[:, None, :] == jnp.arange(devices * capacity, dtype=jnp.int32)[None, :, None]
    pick = pick.astype(jnp.bfloat16)
    send = jnp.einsum(
        "jmt,jtf->mjf",
        pick,
        context.reshape(n_seq, tok_rows, feat),
        preferred_element_type=jnp.float32,
    ).astype(jnp.bfloat16)
    send = send.reshape(devices, slots, feat)
    tags = jnp.einsum(
        "jmt,jt->mj",
        pick,
        (adapter_all.reshape(n_seq, tok_rows) + 1).astype(jnp.bfloat16),
        preferred_element_type=jnp.float32,
    ).reshape(devices, slots) - 1.0
    tag_row = jnp.pad(tags.astype(jnp.bfloat16), ((0, 0), (0, feat - slots)))
    send = jnp.concatenate([send, tag_row[:, None, :]], axis=1)
    got = lax.all_to_all(send, ("seq", "store"), split_axis=0, concat_axis=0, tiled=True)
    got = got.reshape(n_seq, n_store, slots + 1, feat)
    rows = jnp.transpose(got[:, :, :slots, :], (1, 2, 0, 3)).reshape(n_store * slots, width)
    row_tags = got[0, :, slots, :slots].reshape(n_store * slots, 1).astype(jnp.float32)

    low = jnp.dot(rows, adapter_down, preferred_element_type=jnp.float32)
    lane_owner = (jnp.arange(low.shape[1], dtype=jnp.int32) // RANK).astype(jnp.float32)
    low = jnp.where(row_tags == lane_owner[None, :], low, 0.0).astype(jnp.bfloat16)
    delta = jnp.dot(low, adapter_up, preferred_element_type=jnp.float32).astype(jnp.bfloat16)
    mixed_rows = (rows.astype(jnp.float32) + delta.astype(jnp.float32)).astype(jnp.bfloat16)
    ret = jnp.transpose(
        mixed_rows.reshape(n_store, capacity, n_seq, width), (2, 0, 1, 3)
    ).reshape(devices, capacity, width)
    back = lax.all_to_all(ret, ("seq", "store"), split_axis=0, concat_axis=0, tiled=True)
    owners = chosen // EXP_DEV
    placed = owners * capacity + ranks(owners)
    mixed = back.reshape(devices * capacity, width)[placed]
    return mixed[None]


def solution(mesh):
    return jax.shard_map(
        local,
        mesh=mesh,
        in_specs=(
            P("store", "seq", None),
            P("store", "seq", None),
            P("store", "seq", None),
            P("store", "seq"),
            P("store", "seq"),
            P(None, ("seq", "store")),
            P(("seq", "store"), None),
        ),
        out_specs=P("store", "seq", None),
        check_vma=False,
    )
```

```python
import functools

import jax
import jax.numpy as jnp
from jax import lax
from jax.experimental import pallas as pl
from jax.experimental.pallas import tpu as pltpu
from jax.sharding import PartitionSpec as P

HEAD_DIM = 128
HEADS = 32
KV_HEADS = 4
RANK = 64
EXP_DEV = 16
MAX_DOC = 2048


def _attn_kernel(lo_ref, full_ref, q_ref, kt_ref, v_ref, qs_ref, o_ref, *, bq, bk, rc, scale):
    i = pl.program_id(0)
    lanes = 128
    lo = lo_ref[i]
    mid = jnp.clip(full_ref[i], lo, i)

    for r in range(bq // rc):
        rows = pl.ds(r * rc, rc)
        q = q_ref[rows, :]
        qs = qs_ref[rows, :]
        qpos = i * bq + r * rc + lax.broadcasted_iota(jnp.int32, (rc, 1), 0)

        def raw(kb, q=q):
            start = pl.multiple_of(kb * bk, bk)
            s = jnp.dot(q, kt_ref[:, pl.ds(start, bk)], preferred_element_type=jnp.float32)
            return s * scale, start

        def masked(kb, raw=raw, qs=qs, qpos=qpos):
            s, start = raw(kb)
            kpos = start + lax.broadcasted_iota(jnp.int32, (1, bk), 1)
            ok = (kpos >= qs) & (kpos <= qpos)
            return jnp.where(ok, s, jnp.float32(-1e30)), start

        def fold_max(m, s):
            for c in range(bk // lanes):
                m = jnp.maximum(m, s[:, c * lanes : (c + 1) * lanes])
            return m

        m = jnp.full((rc, lanes), -1e30, jnp.float32)
        m = lax.fori_loop(lo, mid, lambda kb, m, f=masked: fold_max(m, f(kb)[0]), m)
        m = lax.fori_loop(mid, i, lambda kb, m, f=raw: fold_max(m, f(kb)[0]), m)
        m = fold_max(m, masked(i)[0])
        top = jnp.max(m, axis=1, keepdims=True)

        def accum(carry, s, start, top=top):
            tot, acc = carry
            p = jnp.exp(s - top)
            for c in range(bk // lanes):
                tot = tot + p[:, c * lanes : (c + 1) * lanes]
            v = v_ref[pl.ds(start, bk), :]
            acc = acc + jnp.dot(p.astype(jnp.bfloat16), v, preferred_element_type=jnp.float32)
            return tot, acc

        carry = (jnp.zeros((rc, lanes), jnp.float32), jnp.zeros((rc, q.shape[1]), jnp.float32))
        carry = lax.fori_loop(lo, mid, lambda kb, c, f=masked, a=accum: a(c, *f(kb)), carry)
        carry = lax.fori_loop(mid, i, lambda kb, c, f=raw, a=accum: a(c, *f(kb)), carry)
        tot, acc = accum(carry, *masked(i))
        total = jnp.sum(tot, axis=1, keepdims=True)
        o_ref[rows, :] = (acc / total).astype(o_ref.dtype)


def attend(queries, key_rows, value_rows, segments):
    length, dim = key_rows.shape
    bq = min(512, length)
    bk = min(512, length)
    n_q = length // bq
    pos = jnp.arange(length, dtype=jnp.int32)
    boundary = jnp.concatenate(
        [jnp.ones((1,), jnp.bool_), segments[1:] != segments[:-1]]
    )
    doc_start = lax.cummax(jnp.where(boundary, pos, 0), axis=0)
    lo_blk = doc_start[::bq] // bk
    full_blk = (doc_start[bq - 1 :: bq] + bk - 1) // bk
    q_rows = queries.reshape(length, dim)
    kernel = functools.partial(_attn_kernel, bq=bq, bk=bk, rc=bq, scale=dim ** (-0.5))
    out = pl.pallas_call(
        kernel,
        out_shape=jax.ShapeDtypeStruct((length, dim), jnp.bfloat16),
        grid_spec=pltpu.PrefetchScalarGridSpec(
            num_scalar_prefetch=2,
            grid=(n_q,),
            in_specs=[
                pl.BlockSpec((bq, dim), lambda i, lo, full: (i, 0)),
                pl.BlockSpec((dim, length), lambda i, lo, full: (0, 0)),
                pl.BlockSpec((length, dim), lambda i, lo, full: (0, 0)),
                pl.BlockSpec((bq, 1), lambda i, lo, full: (i, 0)),
            ],
            out_specs=pl.BlockSpec((bq, dim), lambda i, lo, full: (i, 0)),
        ),
        cost_estimate=pl.CostEstimate(
            flops=6 * length * MAX_DOC * dim,
            transcendentals=length * MAX_DOC,
            bytes_accessed=8 * length * dim,
        ),
    )(lo_blk, full_blk, q_rows, key_rows.T, value_rows, doc_start.reshape(length, 1))
    return out


def local(queries, keys, values, segment_ids, route_ids, adapter_down, adapter_up):
    n_seq = lax.axis_size("seq")
    n_store = lax.axis_size("store")
    tok_rows = queries.shape[1]
    width = queries.shape[2]
    length = tok_rows * n_seq
    heads_here = HEADS // n_seq
    feat = heads_here * HEAD_DIM
    group = HEADS // KV_HEADS
    devices = n_seq * n_store
    capacity = max(2, 2 * tok_rows // devices)
    slots = n_seq * capacity

    q_send = queries[0].reshape(tok_rows, n_seq, feat)
    paired = jnp.concatenate(
        [keys[0].reshape(tok_rows, KV_HEADS, HEAD_DIM), values[0].reshape(tok_rows, KV_HEADS, HEAD_DIM)],
        axis=2,
    )
    kv_send = jnp.take(paired, (jnp.arange(n_seq) * heads_here) // group, axis=1)
    chosen = route_ids[0]
    meta = jnp.concatenate(
        [segment_ids[0], chosen // EXP_DEV, chosen % EXP_DEV]
    ).astype(jnp.bfloat16)
    meta_w = feat + 2 * HEAD_DIM
    meta = jnp.pad(meta, (0, meta_w - meta.shape[0]))
    payload = jnp.concatenate(
        [
            jnp.concatenate([q_send, kv_send], axis=2),
            jnp.broadcast_to(meta[None, None, :], (1, n_seq, meta_w)),
        ],
        axis=0,
    )
    got_in = lax.all_to_all(payload, "seq", split_axis=1, concat_axis=0, tiled=True)
    got_in = got_in.reshape(n_seq, tok_rows + 1, meta_w)
    q_all = got_in[:, :tok_rows, :feat].reshape(length, heads_here, HEAD_DIM)
    k_all = got_in[:, :tok_rows, feat : feat + HEAD_DIM].reshape(length, HEAD_DIM)
    v_all = got_in[:, :tok_rows, feat + HEAD_DIM :].reshape(length, HEAD_DIM)
    meta_all = got_in[:, tok_rows, : 3 * tok_rows].astype(jnp.int32)
    segments = meta_all[:, :tok_rows].reshape(length)
    owner_all = meta_all[:, tok_rows : 2 * tok_rows]
    adapter_all = meta_all[:, 2 * tok_rows :]

    context = attend(q_all, k_all, v_all, segments).reshape(length, feat)

    def ranks(owner_rows):
        one_hot = (owner_rows[..., None] == jnp.arange(devices, dtype=jnp.int32)).astype(jnp.int32)
        return jnp.sum(jnp.cumsum(one_hot, axis=-2) * one_hot, axis=-1) - 1

    pick = (
        owner_all * capacity + ranks(owner_all)
    )[:, None, :] == jnp.arange(devices * capacity, dtype=jnp.int32)[None, :, None]
    pick = pick.astype(jnp.bfloat16)
    send = jnp.einsum(
        "jmt,jtf->mjf",
        pick,
        context.reshape(n_seq, tok_rows, feat),
        preferred_element_type=jnp.float32,
    ).astype(jnp.bfloat16)
    send = send.reshape(devices, slots, feat)
    tags = jnp.einsum(
        "jmt,jt->mj",
        pick,
        (adapter_all.reshape(n_seq, tok_rows) + 1).astype(jnp.bfloat16),
        preferred_element_type=jnp.float32,
    ).reshape(devices, slots) - 1.0
    tag_row = jnp.pad(tags.astype(jnp.bfloat16), ((0, 0), (0, feat - slots)))
    send = jnp.concatenate([send, tag_row[:, None, :]], axis=1)
    got = lax.all_to_all(send, ("seq", "store"), split_axis=0, concat_axis=0, tiled=True)
    got = got.reshape(n_seq, n_store, slots + 1, feat)
    rows = jnp.transpose(got[:, :, :slots, :], (1, 2, 0, 3)).reshape(n_store * slots, width)
    row_tags = got[0, :, slots, :slots].reshape(n_store * slots, 1).astype(jnp.float32)

    low = jnp.dot(rows, adapter_down, preferred_element_type=jnp.float32)
    lane_owner = (jnp.arange(low.shape[1], dtype=jnp.int32) // RANK).astype(jnp.float32)
    low = jnp.where(row_tags == lane_owner[None, :], low, 0.0).astype(jnp.bfloat16)
    delta = jnp.dot(low, adapter_up, preferred_element_type=jnp.float32).astype(jnp.bfloat16)
    mixed_rows = (rows.astype(jnp.float32) + delta.astype(jnp.float32)).astype(jnp.bfloat16)
    ret = jnp.transpose(
        mixed_rows.reshape(n_store, capacity, n_seq, width), (2, 0, 1, 3)
    ).reshape(devices, capacity, width)
    back = lax.all_to_all(ret, ("seq", "store"), split_axis=0, concat_axis=0, tiled=True)
    owners = chosen // EXP_DEV
    placed = owners * capacity + ranks(owners)
    mixed = back.reshape(devices * capacity, width)[placed]
    return mixed[None]


def solution(mesh):
    return jax.shard_map(
        local,
        mesh=mesh,
        in_specs=(
            P("store", "seq", None),
            P("store", "seq", None),
            P("store", "seq", None),
            P("store", "seq"),
            P("store", "seq"),
            P(None, ("seq", "store")),
            P(("seq", "store"), None),
        ),
        out_specs=P("store", "seq", None),
        check_vma=False,
    )
```

```python
import functools

import jax
import jax.numpy as jnp
from jax import lax
from jax.experimental import pallas as pl
from jax.experimental.pallas import tpu as pltpu
from jax.sharding import PartitionSpec as P

HEAD_DIM = 128
HEADS = 32
KV_HEADS = 4
RANK = 64
EXP_DEV = 16
MAX_DOC = 2048
N_DOCS = 4


def _attn_kernel(lo_ref, full_ref, bnd_ref, q_ref, kt_ref, v_ref, o_ref, *, bq, bk, rc, scale):
    i = pl.program_id(0)
    lanes = 128
    lo = lo_ref[i]
    mid = jnp.clip(full_ref[i], lo, i)

    for r in range(bq // rc):
        rows = pl.ds(r * rc, rc)
        q = q_ref[rows, :]
        qpos = i * bq + r * rc + lax.broadcasted_iota(jnp.int32, (rc, 1), 0)
        qs = jnp.zeros((rc, 1), jnp.int32)
        for c in range(N_DOCS - 1):
            qs = jnp.where(qpos >= bnd_ref[c], bnd_ref[c], qs)

        def raw(kb, q=q):
            start = pl.multiple_of(kb * bk, bk)
            s = jnp.dot(q, kt_ref[:, pl.ds(start, bk)], preferred_element_type=jnp.float32)
            return s * scale, start

        def masked(kb, raw=raw, qs=qs, qpos=qpos):
            s, start = raw(kb)
            kpos = start + lax.broadcasted_iota(jnp.int32, (1, bk), 1)
            ok = (kpos >= qs) & (kpos <= qpos)
            return jnp.where(ok, s, jnp.float32(-1e30)), start

        def fold_max(m, s):
            for c in range(bk // lanes):
                m = jnp.maximum(m, s[:, c * lanes : (c + 1) * lanes])
            return m

        m = jnp.full((rc, lanes), -1e30, jnp.float32)
        m = lax.fori_loop(lo, mid, lambda kb, m, f=masked: fold_max(m, f(kb)[0]), m)
        m = lax.fori_loop(mid, i, lambda kb, m, f=raw: fold_max(m, f(kb)[0]), m)
        m = fold_max(m, masked(i)[0])
        top = jnp.max(m, axis=1, keepdims=True)

        def accum(carry, s, start, top=top):
            tot, acc = carry
            p = jnp.exp(s - top)
            for c in range(bk // lanes):
                tot = tot + p[:, c * lanes : (c + 1) * lanes]
            v = v_ref[pl.ds(start, bk), :]
            acc = acc + jnp.dot(p.astype(jnp.bfloat16), v, preferred_element_type=jnp.float32)
            return tot, acc

        carry = (jnp.zeros((rc, lanes), jnp.float32), jnp.zeros((rc, q.shape[1]), jnp.float32))
        carry = lax.fori_loop(lo, mid, lambda kb, c, f=masked, a=accum: a(c, *f(kb)), carry)
        carry = lax.fori_loop(mid, i, lambda kb, c, f=raw, a=accum: a(c, *f(kb)), carry)
        tot, acc = accum(carry, *masked(i))
        total = jnp.sum(tot, axis=1, keepdims=True)
        o_ref[rows, :] = (acc / total).astype(o_ref.dtype)


def attend(queries, key_rows, value_rows, segments):
    length, dim = key_rows.shape
    bq = min(512, length)
    bk = min(512, length)
    n_q = length // bq
    bounds = jnp.sum(
        segments[None, :] < jnp.arange(1, N_DOCS, dtype=jnp.int32)[:, None], axis=1
    ).astype(jnp.int32)

    def doc_start_at(t):
        first = jnp.zeros_like(t)
        for c in range(N_DOCS - 1):
            first = jnp.where(t >= bounds[c], bounds[c], first)
        return first

    firsts = jnp.arange(n_q, dtype=jnp.int32) * bq
    lo_blk = doc_start_at(firsts) // bk
    full_blk = (doc_start_at(firsts + bq - 1) + bk - 1) // bk
    q_rows = queries.reshape(length, dim)
    kernel = functools.partial(_attn_kernel, bq=bq, bk=bk, rc=bq, scale=dim ** (-0.5))
    out = pl.pallas_call(
        kernel,
        out_shape=jax.ShapeDtypeStruct((length, dim), jnp.bfloat16),
        grid_spec=pltpu.PrefetchScalarGridSpec(
            num_scalar_prefetch=3,
            grid=(n_q,),
            in_specs=[
                pl.BlockSpec((bq, dim), lambda i, lo, full, bnd: (i, 0)),
                pl.BlockSpec((dim, length), lambda i, lo, full, bnd: (0, 0)),
                pl.BlockSpec((length, dim), lambda i, lo, full, bnd: (0, 0)),
            ],
            out_specs=pl.BlockSpec((bq, dim), lambda i, lo, full, bnd: (i, 0)),
        ),
        cost_estimate=pl.CostEstimate(
            flops=6 * length * MAX_DOC * dim,
            transcendentals=length * MAX_DOC,
            bytes_accessed=8 * length * dim,
        ),
    )(lo_blk, full_blk, bounds, q_rows, key_rows.T, value_rows)
    return out


def local(queries, keys, values, segment_ids, route_ids, adapter_down, adapter_up):
    n_seq = lax.axis_size("seq")
    n_store = lax.axis_size("store")
    tok_rows = queries.shape[1]
    width = queries.shape[2]
    length = tok_rows * n_seq
    heads_here = HEADS // n_seq
    feat = heads_here * HEAD_DIM
    group = HEADS // KV_HEADS
    devices = n_seq * n_store
    capacity = max(2, 2 * tok_rows // devices)
    slots = n_seq * capacity

    q_send = queries[0].reshape(tok_rows, n_seq, feat)
    paired = jnp.concatenate(
        [keys[0].reshape(tok_rows, KV_HEADS, HEAD_DIM), values[0].reshape(tok_rows, KV_HEADS, HEAD_DIM)],
        axis=2,
    )
    kv_send = jnp.take(paired, (jnp.arange(n_seq) * heads_here) // group, axis=1)
    chosen = route_ids[0]
    owners = chosen // EXP_DEV
    one_hot = (owners[:, None] == jnp.arange(devices, dtype=jnp.int32)[None, :]).astype(jnp.int32)
    rank = jnp.sum(jnp.cumsum(one_hot, axis=0) * one_hot, axis=1) - 1
    code = owners * capacity + rank
    meta = jnp.concatenate([segment_ids[0], code, chosen % EXP_DEV]).astype(jnp.bfloat16)
    meta_w = feat + 2 * HEAD_DIM
    meta = jnp.pad(meta, (0, meta_w - meta.shape[0]))
    payload = jnp.concatenate(
        [
            jnp.concatenate([q_send, kv_send], axis=2),
            jnp.broadcast_to(meta[None, None, :], (1, n_seq, meta_w)),
        ],
        axis=0,
    )
    got_in = lax.all_to_all(payload, "seq", split_axis=1, concat_axis=0, tiled=True)
    got_in = got_in.reshape(n_seq, tok_rows + 1, meta_w)
    q_all = got_in[:, :tok_rows, :feat].reshape(length, heads_here, HEAD_DIM)
    k_all = got_in[:, :tok_rows, feat : feat + HEAD_DIM].reshape(length, HEAD_DIM)
    v_all = got_in[:, :tok_rows, feat + HEAD_DIM :].reshape(length, HEAD_DIM)
    meta_all = got_in[:, tok_rows, : 3 * tok_rows].astype(jnp.int32)
    segments = meta_all[:, :tok_rows].reshape(length)
    code_all = meta_all[:, tok_rows : 2 * tok_rows]
    adapter_all = meta_all[:, 2 * tok_rows :]

    context = attend(q_all, k_all, v_all, segments).reshape(length, feat)

    pick = code_all[:, None, :] == jnp.arange(devices * capacity, dtype=jnp.int32)[None, :, None]
    pick = pick.astype(jnp.bfloat16)
    send = jnp.einsum(
        "jmt,jtf->mjf",
        pick,
        context.reshape(n_seq, tok_rows, feat),
        preferred_element_type=jnp.float32,
    ).astype(jnp.bfloat16)
    send = send.reshape(devices, slots, feat)
    tags = jnp.einsum(
        "jmt,jt->mj",
        pick,
        (adapter_all.reshape(n_seq, tok_rows) + 1).astype(jnp.bfloat16),
        preferred_element_type=jnp.float32,
    ).reshape(devices, slots) - 1.0
    tag_row = jnp.pad(tags.astype(jnp.bfloat16), ((0, 0), (0, feat - slots)))
    send = jnp.concatenate([send, tag_row[:, None, :]], axis=1)
    got = lax.all_to_all(send, ("seq", "store"), split_axis=0, concat_axis=0, tiled=True)
    got = got.reshape(n_seq, n_store, slots + 1, feat)
    rows = jnp.transpose(
        got[:, :, :slots, :].reshape(n_seq, n_store, capacity, n_seq, feat), (3, 1, 2, 0, 4)
    ).reshape(n_store * slots, width)
    row_tags = jnp.transpose(
        got[0, :, slots, :slots].reshape(n_store, capacity, n_seq), (2, 0, 1)
    ).reshape(n_store * slots, 1).astype(jnp.float32)

    low = jnp.dot(rows, adapter_down, preferred_element_type=jnp.float32)
    lane_owner = (jnp.arange(low.shape[1], dtype=jnp.int32) // RANK).astype(jnp.float32)
    low = jnp.where(row_tags == lane_owner[None, :], low, 0.0).astype(jnp.bfloat16)
    delta = jnp.dot(low, adapter_up, preferred_element_type=jnp.float32).astype(jnp.bfloat16)
    mixed_rows = (rows.astype(jnp.float32) + delta.astype(jnp.float32)).astype(jnp.bfloat16)
    ret = mixed_rows.reshape(devices, capacity, width)
    back = lax.all_to_all(ret, ("seq", "store"), split_axis=0, concat_axis=0, tiled=True)
    mixed = back[owners, rank]
    return mixed[None]


def solution(mesh):
    return jax.shard_map(
        local,
        mesh=mesh,
        in_specs=(
            P("store", "seq", None),
            P("store", "seq", None),
            P("store", "seq", None),
            P("store", "seq"),
            P("store", "seq"),
            P(None, ("seq", "store")),
            P(("seq", "store"), None),
        ),
        out_specs=P("store", "seq", None),
        check_vma=False,
    )
```

```python
import functools

import jax
import jax.numpy as jnp
from jax import lax
from jax.experimental import pallas as pl
from jax.experimental.pallas import tpu as pltpu
from jax.sharding import PartitionSpec as P

HEAD_DIM = 128
HEADS = 32
KV_HEADS = 4
RANK = 64
EXP_DEV = 16
MAX_DOC = 2048
N_DOCS = 4


def _attn_kernel(lo_ref, full_ref, bnd_ref, q_ref, kt_ref, v_ref, o_ref, *, bq, bk, rc, scale):
    i = pl.program_id(0)
    lanes = 128
    lo = lo_ref[i]
    mid = jnp.clip(full_ref[i], lo, i)

    for r in range(bq // rc):
        rows = pl.ds(r * rc, rc)
        q = q_ref[rows, :]
        qpos = i * bq + r * rc + lax.broadcasted_iota(jnp.int32, (rc, 1), 0)
        qs = jnp.zeros((rc, 1), jnp.int32)
        for c in range(N_DOCS - 1):
            qs = jnp.where(qpos >= bnd_ref[c], bnd_ref[c], qs)

        def raw(kb, q=q):
            start = pl.multiple_of(kb * bk, bk)
            s = jnp.dot(q, kt_ref[:, pl.ds(start, bk)], preferred_element_type=jnp.float32)
            return s * scale, start

        def masked(kb, raw=raw, qs=qs, qpos=qpos):
            s, start = raw(kb)
            kpos = start + lax.broadcasted_iota(jnp.int32, (1, bk), 1)
            ok = (kpos >= qs) & (kpos <= qpos)
            return jnp.where(ok, s, jnp.float32(-1e30)), start

        def fold_max(m, s):
            for c in range(bk // lanes):
                m = jnp.maximum(m, s[:, c * lanes : (c + 1) * lanes])
            return m

        m = jnp.full((rc, lanes), -1e30, jnp.float32)
        m = lax.fori_loop(lo, mid, lambda kb, m, f=masked: fold_max(m, f(kb)[0]), m)
        m = lax.fori_loop(mid, i, lambda kb, m, f=raw: fold_max(m, f(kb)[0]), m)
        m = fold_max(m, masked(i)[0])
        top = jnp.max(m, axis=1, keepdims=True)

        def accum(carry, s, start, top=top):
            tot, acc = carry
            p = jnp.exp(s - top)
            for c in range(bk // lanes):
                tot = tot + p[:, c * lanes : (c + 1) * lanes]
            v = v_ref[pl.ds(start, bk), :]
            acc = acc + jnp.dot(p.astype(jnp.bfloat16), v, preferred_element_type=jnp.float32)
            return tot, acc

        carry = (jnp.zeros((rc, lanes), jnp.float32), jnp.zeros((rc, q.shape[1]), jnp.float32))
        carry = lax.fori_loop(lo, mid, lambda kb, c, f=masked, a=accum: a(c, *f(kb)), carry)
        carry = lax.fori_loop(mid, i, lambda kb, c, f=raw, a=accum: a(c, *f(kb)), carry)
        tot, acc = accum(carry, *masked(i))
        total = jnp.sum(tot, axis=1, keepdims=True)
        o_ref[rows, :] = (acc / total).astype(o_ref.dtype)


def attend(queries, key_rows, value_rows, segments):
    length, dim = key_rows.shape
    bq = min(512, length)
    bk = min(512, length)
    n_q = length // bq
    bounds = jnp.sum(
        segments[None, :] < jnp.arange(1, N_DOCS, dtype=jnp.int32)[:, None], axis=1
    ).astype(jnp.int32)

    def doc_start_at(t):
        first = jnp.zeros_like(t)
        for c in range(N_DOCS - 1):
            first = jnp.where(t >= bounds[c], bounds[c], first)
        return first

    firsts = jnp.arange(n_q, dtype=jnp.int32) * bq
    lo_blk = doc_start_at(firsts) // bk
    full_blk = (doc_start_at(firsts + bq - 1) + bk - 1) // bk
    q_rows = queries.reshape(length, dim)
    kernel = functools.partial(_attn_kernel, bq=bq, bk=bk, rc=bq, scale=dim ** (-0.5))
    out = pl.pallas_call(
        kernel,
        out_shape=jax.ShapeDtypeStruct((length, dim), jnp.bfloat16),
        grid_spec=pltpu.PrefetchScalarGridSpec(
            num_scalar_prefetch=3,
            grid=(n_q,),
            in_specs=[
                pl.BlockSpec((bq, dim), lambda i, lo, full, bnd: (i, 0)),
                pl.BlockSpec((dim, length), lambda i, lo, full, bnd: (0, 0)),
                pl.BlockSpec((length, dim), lambda i, lo, full, bnd: (0, 0)),
            ],
            out_specs=pl.BlockSpec((bq, dim), lambda i, lo, full, bnd: (i, 0)),
        ),
        cost_estimate=pl.CostEstimate(
            flops=6 * length * MAX_DOC * dim,
            transcendentals=length * MAX_DOC,
            bytes_accessed=8 * length * dim,
        ),
    )(lo_blk, full_blk, bounds, q_rows, key_rows.T, value_rows)
    return out


def local(queries, keys, values, segment_ids, route_ids, adapter_down, adapter_up):
    n_seq = lax.axis_size("seq")
    n_store = lax.axis_size("store")
    tok_rows = queries.shape[1]
    width = queries.shape[2]
    length = tok_rows * n_seq
    heads_here = HEADS // n_seq
    feat = heads_here * HEAD_DIM
    group = HEADS // KV_HEADS
    devices = n_seq * n_store
    capacity = max(2, 2 * tok_rows // devices)
    slots = n_seq * capacity

    half = tok_rows // 2
    q_send = queries[0].reshape(tok_rows, n_seq, feat)
    paired = jnp.concatenate(
        [keys[0].reshape(tok_rows, KV_HEADS, HEAD_DIM), values[0].reshape(tok_rows, KV_HEADS, HEAD_DIM)],
        axis=2,
    )
    halves = jnp.transpose(paired.reshape(2, half, KV_HEADS, 2 * HEAD_DIM), (0, 2, 1, 3)).reshape(
        2 * KV_HEADS, half, 2 * HEAD_DIM
    )
    dest = jnp.arange(n_seq, dtype=jnp.int32)
    kv_send = jnp.take(halves, (dest % 2) * KV_HEADS + (dest * heads_here) // group, axis=0)
    kv_send = jnp.transpose(kv_send.reshape(n_seq, tok_rows, HEAD_DIM), (1, 0, 2))
    chosen = route_ids[0]
    owners = chosen // EXP_DEV
    one_hot = (owners[:, None] == jnp.arange(devices, dtype=jnp.int32)[None, :]).astype(jnp.int32)
    rank = jnp.sum(jnp.cumsum(one_hot, axis=0) * one_hot, axis=1) - 1
    code = owners * capacity + rank
    meta = jnp.concatenate([segment_ids[0], code, chosen % EXP_DEV]).astype(jnp.bfloat16)
    meta_w = feat + HEAD_DIM
    meta_rows = -(-meta.shape[0] // meta_w)
    meta = jnp.pad(meta, (0, meta_rows * meta_w - meta.shape[0])).reshape(meta_rows, meta_w)
    payload = jnp.concatenate(
        [
            jnp.concatenate([q_send, kv_send], axis=2),
            jnp.broadcast_to(meta[:, None, :], (meta_rows, n_seq, meta_w)),
        ],
        axis=0,
    )
    got_in = lax.all_to_all(payload, "seq", split_axis=1, concat_axis=0, tiled=True)
    got_in = got_in.reshape(n_seq, tok_rows + meta_rows, meta_w)
    q_all = got_in[:, :tok_rows, :feat].reshape(length, heads_here, HEAD_DIM)
    kv_mine = got_in[:, :tok_rows, feat:].reshape(n_seq, half, 2 * HEAD_DIM)
    kv_other = lax.ppermute(kv_mine, "seq", [(i, i ^ 1) for i in range(n_seq)])
    even = lax.axis_index("seq") % 2 == 0
    kv_all = jnp.stack(
        [jnp.where(even, kv_mine, kv_other), jnp.where(even, kv_other, kv_mine)], axis=1
    ).reshape(length, 2 * HEAD_DIM)
    k_all = kv_all[:, :HEAD_DIM]
    v_all = kv_all[:, HEAD_DIM:]
    meta_all = got_in[:, tok_rows:, :].reshape(n_seq, meta_rows * meta_w)[:, : 3 * tok_rows]
    meta_all = meta_all.astype(jnp.int32)
    segments = meta_all[:, :tok_rows].reshape(length)
    code_all = meta_all[:, tok_rows : 2 * tok_rows]
    adapter_all = meta_all[:, 2 * tok_rows :]

    context = attend(q_all, k_all, v_all, segments).reshape(length, feat)

    pick = code_all[:, None, :] == jnp.arange(devices * capacity, dtype=jnp.int32)[None, :, None]
    pick = pick.astype(jnp.bfloat16)
    send = jnp.einsum(
        "jmt,jtf->mjf",
        pick,
        context.reshape(n_seq, tok_rows, feat),
        preferred_element_type=jnp.float32,
    ).astype(jnp.bfloat16)
    send = send.reshape(devices, slots, feat)
    tags = jnp.einsum(
        "jmt,jt->mj",
        pick,
        (adapter_all.reshape(n_seq, tok_rows) + 1).astype(jnp.bfloat16),
        preferred_element_type=jnp.float32,
    ).reshape(devices, slots) - 1.0
    tag_row = jnp.pad(tags.astype(jnp.bfloat16), ((0, 0), (0, feat - slots)))
    send = jnp.concatenate([send, tag_row[:, None, :]], axis=1)
    got = lax.all_to_all(send, ("seq", "store"), split_axis=0, concat_axis=0, tiled=True)
    got = got.reshape(n_seq, n_store, slots + 1, feat)
    rows = jnp.transpose(
        got[:, :, :slots, :].reshape(n_seq, n_store, capacity, n_seq, feat), (3, 1, 2, 0, 4)
    ).reshape(n_store * slots, width)
    row_tags = jnp.transpose(
        got[0, :, slots, :slots].reshape(n_store, capacity, n_seq), (2, 0, 1)
    ).reshape(n_store * slots, 1).astype(jnp.float32)

    low = jnp.dot(rows, adapter_down, preferred_element_type=jnp.float32)
    lane_owner = (jnp.arange(low.shape[1], dtype=jnp.int32) // RANK).astype(jnp.float32)
    low = jnp.where(row_tags == lane_owner[None, :], low, 0.0).astype(jnp.bfloat16)
    delta = jnp.dot(low, adapter_up, preferred_element_type=jnp.float32).astype(jnp.bfloat16)
    mixed_rows = (rows.astype(jnp.float32) + delta.astype(jnp.float32)).astype(jnp.bfloat16)
    ret = mixed_rows.reshape(devices, capacity, width)
    back = lax.all_to_all(ret, ("seq", "store"), split_axis=0, concat_axis=0, tiled=True)
    mixed = back[owners, rank]
    return mixed[None]


def solution(mesh):
    return jax.shard_map(
        local,
        mesh=mesh,
        in_specs=(
            P("store", "seq", None),
            P("store", "seq", None),
            P("store", "seq", None),
            P("store", "seq"),
            P("store", "seq"),
            P(None, ("seq", "store")),
            P(("seq", "store"), None),
        ),
        out_specs=P("store", "seq", None),
        check_vma=False,
    )
```

```python
import functools

import jax
import jax.numpy as jnp
from jax import lax
from jax.experimental import pallas as pl
from jax.experimental.pallas import tpu as pltpu
from jax.sharding import PartitionSpec as P

HEAD_DIM = 128
HEADS = 32
KV_HEADS = 4
RANK = 64
EXP_DEV = 16
MAX_DOC = 2048
N_DOCS = 4


def _attn_kernel(lo_ref, full_ref, bnd_ref, q_ref, kt_ref, v_ref, o_ref, s_ref, *, bq, bk, scale):
    i = pl.program_id(0)
    lanes = 128
    nb = s_ref.shape[0]
    lo = jnp.maximum(lo_ref[i], i - (nb - 1))
    mid = jnp.clip(full_ref[i], lo, i)
    q = q_ref[...]
    qpos = i * bq + lax.broadcasted_iota(jnp.int32, (bq, 1), 0)
    qs = jnp.zeros((bq, 1), jnp.int32)
    for c in range(N_DOCS - 1):
        qs = jnp.where(qpos >= bnd_ref[c], bnd_ref[c], qs)

    def raw(kb):
        start = pl.multiple_of(kb * bk, bk)
        s = jnp.dot(q, kt_ref[:, pl.ds(start, bk)], preferred_element_type=jnp.float32)
        return s * scale, start

    def masked(kb):
        s, start = raw(kb)
        kpos = start + lax.broadcasted_iota(jnp.int32, (1, bk), 1)
        ok = (kpos >= qs) & (kpos <= qpos)
        return jnp.where(ok, s, jnp.float32(-1e30)), start

    def keep(kb, m, s):
        s_ref[kb - lo] = s
        for c in range(bk // lanes):
            m = jnp.maximum(m, s[:, c * lanes : (c + 1) * lanes])
        return m

    m = jnp.full((bq, lanes), -1e30, jnp.float32)
    m = lax.fori_loop(lo, mid, lambda kb, m: keep(kb, m, masked(kb)[0]), m)
    m = lax.fori_loop(mid, i, lambda kb, m: keep(kb, m, raw(kb)[0]), m)
    m = keep(i, m, masked(i)[0])
    top = jnp.max(m, axis=1, keepdims=True)

    def accum(kb, carry):
        tot, acc = carry
        p = jnp.exp(s_ref[kb - lo] - top)
        for c in range(bk // lanes):
            tot = tot + p[:, c * lanes : (c + 1) * lanes]
        v = v_ref[pl.ds(pl.multiple_of(kb * bk, bk), bk), :]
        acc = acc + jnp.dot(p.astype(jnp.bfloat16), v, preferred_element_type=jnp.float32)
        return tot, acc

    carry = (jnp.zeros((bq, lanes), jnp.float32), jnp.zeros((bq, q.shape[1]), jnp.float32))
    tot, acc = lax.fori_loop(lo, i + 1, accum, carry)
    total = jnp.sum(tot, axis=1, keepdims=True)
    o_ref[...] = (acc / total).astype(o_ref.dtype)


def attend(queries, key_rows, value_rows, segments):
    length, dim = key_rows.shape
    bq = min(512, length)
    bk = min(512, length)
    n_q = length // bq
    bounds = jnp.sum(
        segments[None, :] < jnp.arange(1, N_DOCS, dtype=jnp.int32)[:, None], axis=1
    ).astype(jnp.int32)

    def doc_start_at(t):
        first = jnp.zeros_like(t)
        for c in range(N_DOCS - 1):
            first = jnp.where(t >= bounds[c], bounds[c], first)
        return first

    firsts = jnp.arange(n_q, dtype=jnp.int32) * bq
    lo_blk = doc_start_at(firsts) // bk
    full_blk = (doc_start_at(firsts + bq - 1) + bk - 1) // bk
    q_rows = queries.reshape(length, dim)
    kernel = functools.partial(_attn_kernel, bq=bq, bk=bk, scale=dim ** (-0.5))
    band = (MAX_DOC + bq - 1) // bk + 1
    out = pl.pallas_call(
        kernel,
        out_shape=jax.ShapeDtypeStruct((length, dim), jnp.bfloat16),
        grid_spec=pltpu.PrefetchScalarGridSpec(
            num_scalar_prefetch=3,
            grid=(n_q,),
            in_specs=[
                pl.BlockSpec((bq, dim), lambda i, lo, full, bnd: (i, 0)),
                pl.BlockSpec((dim, length), lambda i, lo, full, bnd: (0, 0)),
                pl.BlockSpec((length, dim), lambda i, lo, full, bnd: (0, 0)),
            ],
            out_specs=pl.BlockSpec((bq, dim), lambda i, lo, full, bnd: (i, 0)),
            scratch_shapes=[pltpu.VMEM((min(band, n_q), bq, bk), jnp.float32)],
        ),
        compiler_params=pltpu.CompilerParams(vmem_limit_bytes=48 * 1024 * 1024),
        cost_estimate=pl.CostEstimate(
            flops=6 * length * MAX_DOC * dim,
            transcendentals=length * MAX_DOC,
            bytes_accessed=8 * length * dim,
        ),
    )(lo_blk, full_blk, bounds, q_rows, key_rows.T, value_rows)
    return out


def local(queries, keys, values, segment_ids, route_ids, adapter_down, adapter_up):
    n_seq = lax.axis_size("seq")
    n_store = lax.axis_size("store")
    tok_rows = queries.shape[1]
    width = queries.shape[2]
    length = tok_rows * n_seq
    heads_here = HEADS // n_seq
    feat = heads_here * HEAD_DIM
    group = HEADS // KV_HEADS
    devices = n_seq * n_store
    capacity = max(2, 2 * tok_rows // devices)
    slots = n_seq * capacity

    half = tok_rows // 2
    q_send = queries[0].reshape(tok_rows, n_seq, feat)
    paired = jnp.concatenate(
        [keys[0].reshape(tok_rows, KV_HEADS, HEAD_DIM), values[0].reshape(tok_rows, KV_HEADS, HEAD_DIM)],
        axis=2,
    )
    halves = jnp.transpose(paired.reshape(2, half, KV_HEADS, 2 * HEAD_DIM), (0, 2, 1, 3)).reshape(
        2 * KV_HEADS, half, 2 * HEAD_DIM
    )
    dest = jnp.arange(n_seq, dtype=jnp.int32)
    kv_send = jnp.take(halves, (dest % 2) * KV_HEADS + (dest * heads_here) // group, axis=0)
    kv_send = jnp.transpose(kv_send.reshape(n_seq, tok_rows, HEAD_DIM), (1, 0, 2))
    chosen = route_ids[0]
    owners = chosen // EXP_DEV
    one_hot = (owners[:, None] == jnp.arange(devices, dtype=jnp.int32)[None, :]).astype(jnp.int32)
    rank = jnp.sum(jnp.cumsum(one_hot, axis=0) * one_hot, axis=1) - 1
    code = owners * capacity + rank
    meta = jnp.concatenate([segment_ids[0], code, chosen % EXP_DEV]).astype(jnp.bfloat16)
    meta_w = feat + HEAD_DIM
    meta_rows = -(-meta.shape[0] // meta_w)
    meta = jnp.pad(meta, (0, meta_rows * meta_w - meta.shape[0])).reshape(meta_rows, meta_w)
    payload = jnp.concatenate(
        [
            jnp.concatenate([q_send, kv_send], axis=2),
            jnp.broadcast_to(meta[:, None, :], (meta_rows, n_seq, meta_w)),
        ],
        axis=0,
    )
    got_in = lax.all_to_all(payload, "seq", split_axis=1, concat_axis=0, tiled=True)
    got_in = got_in.reshape(n_seq, tok_rows + meta_rows, meta_w)
    q_all = got_in[:, :tok_rows, :feat].reshape(length, heads_here, HEAD_DIM)
    kv_mine = got_in[:, :tok_rows, feat:].reshape(n_seq, half, 2 * HEAD_DIM)
    kv_other = lax.ppermute(kv_mine, "seq", [(i, i ^ 1) for i in range(n_seq)])
    even = lax.axis_index("seq") % 2 == 0
    kv_all = jnp.stack(
        [jnp.where(even, kv_mine, kv_other), jnp.where(even, kv_other, kv_mine)], axis=1
    ).reshape(length, 2 * HEAD_DIM)
    k_all = kv_all[:, :HEAD_DIM]
    v_all = kv_all[:, HEAD_DIM:]
    meta_all = got_in[:, tok_rows:, :].reshape(n_seq, meta_rows * meta_w)[:, : 3 * tok_rows]
    meta_all = meta_all.astype(jnp.int32)
    segments = meta_all[:, :tok_rows].reshape(length)
    code_all = meta_all[:, tok_rows : 2 * tok_rows]
    adapter_all = meta_all[:, 2 * tok_rows :]

    context = attend(q_all, k_all, v_all, segments).reshape(length, feat)

    pick = code_all[:, None, :] == jnp.arange(devices * capacity, dtype=jnp.int32)[None, :, None]
    pick = pick.astype(jnp.bfloat16)
    send = jnp.einsum(
        "jmt,jtf->mjf",
        pick,
        context.reshape(n_seq, tok_rows, feat),
        preferred_element_type=jnp.float32,
    ).astype(jnp.bfloat16)
    send = send.reshape(devices, slots, feat)
    tags = jnp.einsum(
        "jmt,jt->mj",
        pick,
        (adapter_all.reshape(n_seq, tok_rows) + 1).astype(jnp.bfloat16),
        preferred_element_type=jnp.float32,
    ).reshape(devices, slots) - 1.0
    tag_row = jnp.pad(tags.astype(jnp.bfloat16), ((0, 0), (0, feat - slots)))
    send = jnp.concatenate([send, tag_row[:, None, :]], axis=1)
    got = lax.all_to_all(send, ("seq", "store"), split_axis=0, concat_axis=0, tiled=True)
    got = got.reshape(n_seq, n_store, slots + 1, feat)
    rows = jnp.transpose(
        got[:, :, :slots, :].reshape(n_seq, n_store, capacity, n_seq, feat), (3, 1, 2, 0, 4)
    ).reshape(n_store * slots, width)
    row_tags = jnp.transpose(
        got[0, :, slots, :slots].reshape(n_store, capacity, n_seq), (2, 0, 1)
    ).reshape(n_store * slots, 1).astype(jnp.float32)

    low = jnp.dot(rows, adapter_down, preferred_element_type=jnp.float32)
    lane_owner = (jnp.arange(low.shape[1], dtype=jnp.int32) // RANK).astype(jnp.float32)
    low = jnp.where(row_tags == lane_owner[None, :], low, 0.0).astype(jnp.bfloat16)
    delta = jnp.dot(low, adapter_up, preferred_element_type=jnp.float32).astype(jnp.bfloat16)
    mixed_rows = (rows.astype(jnp.float32) + delta.astype(jnp.float32)).astype(jnp.bfloat16)
    ret = mixed_rows.reshape(devices, capacity, width)
    back = lax.all_to_all(ret, ("seq", "store"), split_axis=0, concat_axis=0, tiled=True)
    mixed = back[owners, rank]
    return mixed[None]


def solution(mesh):
    return jax.shard_map(
        local,
        mesh=mesh,
        in_specs=(
            P("store", "seq", None),
            P("store", "seq", None),
            P("store", "seq", None),
            P("store", "seq"),
            P("store", "seq"),
            P(None, ("seq", "store")),
            P(("seq", "store"), None),
        ),
        out_specs=P("store", "seq", None),
        check_vma=False,
    )
```

```python
import functools

import jax
import jax.numpy as jnp
from jax import lax
from jax.experimental import pallas as pl
from jax.experimental.pallas import tpu as pltpu
from jax.sharding import PartitionSpec as P

HEAD_DIM = 128
HEADS = 32
KV_HEADS = 4
RANK = 64
EXP_DEV = 16
MAX_DOC = 2048
N_DOCS = 4


def _attn_kernel(lo_ref, full_ref, bnd_ref, q_ref, kt_ref, v_ref, o_ref, s_ref, *, bq, bk, first, scale):
    i = pl.program_id(0) + first
    lanes = 128
    nb = s_ref.shape[0]
    lo = jnp.maximum(lo_ref[i], i - (nb - 1))
    mid = jnp.clip(full_ref[i], lo, i)
    q = q_ref[...]
    qpos = i * bq + lax.broadcasted_iota(jnp.int32, (bq, 1), 0)
    qs = jnp.zeros((bq, 1), jnp.int32)
    for c in range(N_DOCS - 1):
        qs = jnp.where(qpos >= bnd_ref[c], bnd_ref[c], qs)

    def raw(kb):
        start = pl.multiple_of(kb * bk, bk)
        s = jnp.dot(q, kt_ref[:, pl.ds(start, bk)], preferred_element_type=jnp.float32)
        return s * scale, start

    def masked(kb):
        s, start = raw(kb)
        kpos = start + lax.broadcasted_iota(jnp.int32, (1, bk), 1)
        ok = (kpos >= qs) & (kpos <= qpos)
        return jnp.where(ok, s, jnp.float32(-1e30)), start

    def keep(kb, m, s):
        s_ref[kb - lo] = s
        for c in range(bk // lanes):
            m = jnp.maximum(m, s[:, c * lanes : (c + 1) * lanes])
        return m

    m = jnp.full((bq, lanes), -1e30, jnp.float32)
    m = lax.fori_loop(lo, mid, lambda kb, m: keep(kb, m, masked(kb)[0]), m)
    m = lax.fori_loop(mid, i, lambda kb, m: keep(kb, m, raw(kb)[0]), m)
    m = keep(i, m, masked(i)[0])
    top = jnp.max(m, axis=1, keepdims=True)

    def accum(kb, carry):
        tot, acc = carry
        p = jnp.exp(s_ref[kb - lo] - top)
        for c in range(bk // lanes):
            tot = tot + p[:, c * lanes : (c + 1) * lanes]
        v = v_ref[pl.ds(pl.multiple_of(kb * bk, bk), bk), :]
        acc = acc + jnp.dot(p.astype(jnp.bfloat16), v, preferred_element_type=jnp.float32)
        return tot, acc

    carry = (jnp.zeros((bq, lanes), jnp.float32), jnp.zeros((bq, q.shape[1]), jnp.float32))
    tot, acc = lax.fori_loop(lo, i + 1, accum, carry)
    total = jnp.sum(tot, axis=1, keepdims=True)
    o_ref[...] = (acc / total).astype(o_ref.dtype)


def attend(queries, key_rows, value_rows, segments, parts):
    length, dim = key_rows.shape
    bq = min(512, length)
    bk = min(512, length)
    n_q = length // bq
    bounds = jnp.sum(
        segments[None, :] < jnp.arange(1, N_DOCS, dtype=jnp.int32)[:, None], axis=1
    ).astype(jnp.int32)

    def doc_start_at(t):
        first = jnp.zeros_like(t)
        for c in range(N_DOCS - 1):
            first = jnp.where(t >= bounds[c], bounds[c], first)
        return first

    firsts = jnp.arange(n_q, dtype=jnp.int32) * bq
    lo_blk = doc_start_at(firsts) // bk
    full_blk = (doc_start_at(firsts + bq - 1) + bk - 1) // bk
    q_rows = queries.reshape(length, dim)
    key_cols = key_rows.T
    band = (MAX_DOC + bq - 1) // bk + 1
    per = n_q // parts
    outs = []
    for part in range(parts):
        kernel = functools.partial(
            _attn_kernel, bq=bq, bk=bk, first=part * per, scale=dim ** (-0.5)
        )
        outs.append(
            pl.pallas_call(
                kernel,
                out_shape=jax.ShapeDtypeStruct((per * bq, dim), jnp.bfloat16),
                grid_spec=pltpu.PrefetchScalarGridSpec(
                    num_scalar_prefetch=3,
                    grid=(per,),
                    in_specs=[
                        pl.BlockSpec((bq, dim), lambda i, lo, full, bnd, f=part * per: (i + f, 0)),
                        pl.BlockSpec((dim, length), lambda i, lo, full, bnd: (0, 0)),
                        pl.BlockSpec((length, dim), lambda i, lo, full, bnd: (0, 0)),
                    ],
                    out_specs=pl.BlockSpec((bq, dim), lambda i, lo, full, bnd: (i, 0)),
                    scratch_shapes=[pltpu.VMEM((min(band, n_q), bq, bk), jnp.float32)],
                ),
                compiler_params=pltpu.CompilerParams(vmem_limit_bytes=48 * 1024 * 1024),
                cost_estimate=pl.CostEstimate(
                    flops=6 * per * bq * MAX_DOC * dim,
                    transcendentals=per * bq * MAX_DOC,
                    bytes_accessed=(2 * per * bq + 2 * length) * dim * 2,
                ),
            )(lo_blk, full_blk, bounds, q_rows, key_cols, value_rows)
        )
    return outs


def local(queries, keys, values, segment_ids, route_ids, adapter_down, adapter_up):
    n_seq = lax.axis_size("seq")
    n_store = lax.axis_size("store")
    tok_rows = queries.shape[1]
    width = queries.shape[2]
    length = tok_rows * n_seq
    heads_here = HEADS // n_seq
    feat = heads_here * HEAD_DIM
    group = HEADS // KV_HEADS
    devices = n_seq * n_store
    capacity = max(2, 2 * tok_rows // devices)
    slots = n_seq * capacity

    half = tok_rows // 2
    q_send = queries[0].reshape(tok_rows, n_seq, feat)
    paired = jnp.concatenate(
        [keys[0].reshape(tok_rows, KV_HEADS, HEAD_DIM), values[0].reshape(tok_rows, KV_HEADS, HEAD_DIM)],
        axis=2,
    )
    halves = jnp.transpose(paired.reshape(2, half, KV_HEADS, 2 * HEAD_DIM), (0, 2, 1, 3)).reshape(
        2 * KV_HEADS, half, 2 * HEAD_DIM
    )
    dest = jnp.arange(n_seq, dtype=jnp.int32)
    kv_send = jnp.take(halves, (dest % 2) * KV_HEADS + (dest * heads_here) // group, axis=0)
    kv_send = jnp.transpose(kv_send.reshape(n_seq, tok_rows, HEAD_DIM), (1, 0, 2))
    chosen = route_ids[0]
    owners = chosen // EXP_DEV
    one_hot = (owners[:, None] == jnp.arange(devices, dtype=jnp.int32)[None, :]).astype(jnp.int32)
    rank = jnp.sum(jnp.cumsum(one_hot, axis=0) * one_hot, axis=1) - 1
    code = owners * capacity + rank
    meta = jnp.concatenate([segment_ids[0], code, chosen % EXP_DEV]).astype(jnp.bfloat16)
    meta_w = feat + HEAD_DIM
    meta_rows = -(-meta.shape[0] // meta_w)
    meta = jnp.pad(meta, (0, meta_rows * meta_w - meta.shape[0])).reshape(meta_rows, meta_w)
    payload = jnp.concatenate(
        [
            jnp.concatenate([q_send, kv_send], axis=2),
            jnp.broadcast_to(meta[:, None, :], (meta_rows, n_seq, meta_w)),
        ],
        axis=0,
    )
    got_in = lax.all_to_all(payload, "seq", split_axis=1, concat_axis=0, tiled=True)
    got_in = got_in.reshape(n_seq, tok_rows + meta_rows, meta_w)
    q_all = got_in[:, :tok_rows, :feat].reshape(length, heads_here, HEAD_DIM)
    kv_mine = got_in[:, :tok_rows, feat:].reshape(n_seq, half, 2 * HEAD_DIM)
    kv_other = lax.ppermute(kv_mine, "seq", [(i, i ^ 1) for i in range(n_seq)])
    even = lax.axis_index("seq") % 2 == 0
    kv_all = jnp.stack(
        [jnp.where(even, kv_mine, kv_other), jnp.where(even, kv_other, kv_mine)], axis=1
    ).reshape(length, 2 * HEAD_DIM)
    k_all = kv_all[:, :HEAD_DIM]
    v_all = kv_all[:, HEAD_DIM:]
    meta_all = got_in[:, tok_rows:, :].reshape(n_seq, meta_rows * meta_w)[:, : 3 * tok_rows]
    meta_all = meta_all.astype(jnp.int32)
    segments = meta_all[:, :tok_rows].reshape(length)
    code_all = meta_all[:, tok_rows : 2 * tok_rows]
    adapter_all = meta_all[:, 2 * tok_rows :]

    parts = 2
    blocks = n_seq // parts
    contexts = attend(q_all, k_all, v_all, segments, parts)

    def dispatch(part, context):
        codes = code_all[part * blocks : (part + 1) * blocks]
        pick = codes[:, None, :] == jnp.arange(devices * capacity, dtype=jnp.int32)[None, :, None]
        pick = pick.astype(jnp.bfloat16)
        send = jnp.einsum(
            "jmt,jtf->mjf",
            pick,
            context.reshape(blocks, tok_rows, feat),
            preferred_element_type=jnp.float32,
        ).astype(jnp.bfloat16)
        send = send.reshape(devices, capacity * blocks, feat)
        adapters = adapter_all[part * blocks : (part + 1) * blocks]
        tags = jnp.einsum(
            "jmt,jt->mj",
            pick,
            (adapters + 1).astype(jnp.bfloat16),
            preferred_element_type=jnp.float32,
        ).reshape(devices, capacity * blocks) - 1.0
        tag_row = jnp.pad(tags.astype(jnp.bfloat16), ((0, 0), (0, feat - capacity * blocks)))
        send = jnp.concatenate([send, tag_row[:, None, :]], axis=1)
        return lax.all_to_all(send, ("seq", "store"), split_axis=0, concat_axis=0, tiled=True)

    def owner_rows(got):
        got = got.reshape(n_seq, n_store, capacity * blocks + 1, feat)
        rows = jnp.transpose(
            got[:, :, : capacity * blocks, :].reshape(n_seq, n_store, capacity, blocks, feat),
            (3, 1, 2, 0, 4),
        ).reshape(blocks * n_store * capacity, width)
        row_tags = jnp.transpose(
            got[0, :, capacity * blocks, : capacity * blocks].reshape(n_store, capacity, blocks),
            (2, 0, 1),
        ).reshape(blocks * n_store * capacity, 1).astype(jnp.float32)
        low = jnp.dot(rows, adapter_down, preferred_element_type=jnp.float32)
        lane_owner = (jnp.arange(low.shape[1], dtype=jnp.int32) // RANK).astype(jnp.float32)
        low = jnp.where(row_tags == lane_owner[None, :], low, 0.0).astype(jnp.bfloat16)
        delta = jnp.dot(low, adapter_up, preferred_element_type=jnp.float32).astype(jnp.bfloat16)
        return (rows.astype(jnp.float32) + delta.astype(jnp.float32)).astype(jnp.bfloat16)

    gots = [dispatch(part, ctx) for part, ctx in enumerate(contexts)]
    mixed_rows = jnp.concatenate([owner_rows(got) for got in gots], axis=0)
    ret = mixed_rows.reshape(devices, capacity, width)
    back = lax.all_to_all(ret, ("seq", "store"), split_axis=0, concat_axis=0, tiled=True)
    mixed = back[owners, rank]
    return mixed[None]


def solution(mesh):
    return jax.shard_map(
        local,
        mesh=mesh,
        in_specs=(
            P("store", "seq", None),
            P("store", "seq", None),
            P("store", "seq", None),
            P("store", "seq"),
            P("store", "seq"),
            P(None, ("seq", "store")),
            P(("seq", "store"), None),
        ),
        out_specs=P("store", "seq", None),
        check_vma=False,
    )
```

```python
import functools

import jax
import jax.numpy as jnp
from jax import lax
from jax.experimental import pallas as pl
from jax.experimental.pallas import tpu as pltpu
from jax.sharding import PartitionSpec as P

HEAD_DIM = 128
HEADS = 32
KV_HEADS = 4
RANK = 64
EXP_DEV = 16
MAX_DOC = 2048
N_DOCS = 4


def _attn_kernel(lo_ref, full_ref, bnd_ref, q_ref, kt_ref, v_ref, o_ref, s_ref, *, bq, bk, scale):
    i = pl.program_id(0)
    lanes = 128
    nb = s_ref.shape[0]
    lo = jnp.maximum(lo_ref[i], i - (nb - 1))
    mid = jnp.clip(full_ref[i], lo, i)
    q = q_ref[...]
    qpos = i * bq + lax.broadcasted_iota(jnp.int32, (bq, 1), 0)
    qs = jnp.zeros((bq, 1), jnp.int32)
    for c in range(N_DOCS - 1):
        qs = jnp.where(qpos >= bnd_ref[c], bnd_ref[c], qs)

    def raw(kb):
        start = pl.multiple_of(kb * bk, bk)
        s = jnp.dot(q, kt_ref[:, pl.ds(start, bk)], preferred_element_type=jnp.float32)
        return s * scale, start

    def masked(kb):
        s, start = raw(kb)
        kpos = start + lax.broadcasted_iota(jnp.int32, (1, bk), 1)
        ok = (kpos >= qs) & (kpos <= qpos)
        return jnp.where(ok, s, jnp.float32(-1e30)), start

    def keep(kb, m, s):
        s_ref[kb - lo] = s
        for c in range(bk // lanes):
            m = jnp.maximum(m, s[:, c * lanes : (c + 1) * lanes])
        return m

    m = jnp.full((bq, lanes), -1e30, jnp.float32)
    m = lax.fori_loop(lo, mid, lambda kb, m: keep(kb, m, masked(kb)[0]), m)
    m = lax.fori_loop(mid, i, lambda kb, m: keep(kb, m, raw(kb)[0]), m)
    m = keep(i, m, masked(i)[0])
    top = jnp.max(m, axis=1, keepdims=True)

    def accum(kb, carry):
        tot, acc = carry
        p = jnp.exp(s_ref[kb - lo] - top)
        for c in range(bk // lanes):
            tot = tot + p[:, c * lanes : (c + 1) * lanes]
        v = v_ref[pl.ds(pl.multiple_of(kb * bk, bk), bk), :]
        acc = acc + jnp.dot(p.astype(jnp.bfloat16), v, preferred_element_type=jnp.float32)
        return tot, acc

    carry = (jnp.zeros((bq, lanes), jnp.float32), jnp.zeros((bq, q.shape[1]), jnp.float32))
    tot, acc = lax.fori_loop(lo, i + 1, accum, carry)
    total = jnp.sum(tot, axis=1, keepdims=True)
    o_ref[...] = (acc / total).astype(o_ref.dtype)


def attend(queries, key_rows, value_rows, segments):
    length, dim = key_rows.shape
    bq = min(512, length)
    bk = min(512, length)
    n_q = length // bq
    bounds = jnp.sum(
        segments[None, :] < jnp.arange(1, N_DOCS, dtype=jnp.int32)[:, None], axis=1
    ).astype(jnp.int32)

    def doc_start_at(t):
        first = jnp.zeros_like(t)
        for c in range(N_DOCS - 1):
            first = jnp.where(t >= bounds[c], bounds[c], first)
        return first

    firsts = jnp.arange(n_q, dtype=jnp.int32) * bq
    lo_blk = doc_start_at(firsts) // bk
    full_blk = (doc_start_at(firsts + bq - 1) + bk - 1) // bk
    q_rows = queries.reshape(length, dim)
    kernel = functools.partial(_attn_kernel, bq=bq, bk=bk, scale=dim ** (-0.5))
    band = (MAX_DOC + bq - 1) // bk + 1
    out = pl.pallas_call(
        kernel,
        out_shape=jax.ShapeDtypeStruct((length, dim), jnp.bfloat16),
        grid_spec=pltpu.PrefetchScalarGridSpec(
            num_scalar_prefetch=3,
            grid=(n_q,),
            in_specs=[
                pl.BlockSpec((bq, dim), lambda i, lo, full, bnd: (i, 0)),
                pl.BlockSpec((dim, length), lambda i, lo, full, bnd: (0, 0)),
                pl.BlockSpec((length, dim), lambda i, lo, full, bnd: (0, 0)),
            ],
            out_specs=pl.BlockSpec((bq, dim), lambda i, lo, full, bnd: (i, 0)),
            scratch_shapes=[pltpu.VMEM((min(band, n_q), bq, bk), jnp.float32)],
        ),
        compiler_params=pltpu.CompilerParams(vmem_limit_bytes=48 * 1024 * 1024),
        cost_estimate=pl.CostEstimate(
            flops=6 * length * MAX_DOC * dim,
            transcendentals=length * MAX_DOC,
            bytes_accessed=8 * length * dim,
        ),
    )(lo_blk, full_blk, bounds, q_rows, key_rows.T, value_rows)
    return out


def local(queries, keys, values, segment_ids, route_ids, adapter_down, adapter_up):
    n_seq = lax.axis_size("seq")
    n_store = lax.axis_size("store")
    tok_rows = queries.shape[1]
    width = queries.shape[2]
    length = tok_rows * n_seq
    heads_here = HEADS // n_seq
    feat = heads_here * HEAD_DIM
    group = HEADS // KV_HEADS
    devices = n_seq * n_store
    capacity = max(2, 2 * tok_rows // devices)
    slots = n_seq * capacity

    half = tok_rows // 2
    q_send = jnp.transpose(queries[0].reshape(tok_rows, n_seq, feat), (1, 0, 2))
    paired = jnp.concatenate(
        [keys[0].reshape(tok_rows, KV_HEADS, HEAD_DIM), values[0].reshape(tok_rows, KV_HEADS, HEAD_DIM)],
        axis=2,
    )
    halves = jnp.transpose(paired.reshape(2, half, KV_HEADS, 2 * HEAD_DIM), (0, 2, 1, 3)).reshape(
        2 * KV_HEADS, half, 2 * HEAD_DIM
    )
    dest = jnp.arange(n_seq, dtype=jnp.int32)
    kv_send = jnp.take(halves, (dest % 2) * KV_HEADS + (dest * heads_here) // group, axis=0)
    kv_send = kv_send.reshape(n_seq, tok_rows, HEAD_DIM)
    chosen = route_ids[0]
    owners = chosen // EXP_DEV
    one_hot = (owners[:, None] == jnp.arange(devices, dtype=jnp.int32)[None, :]).astype(jnp.int32)
    rank = jnp.sum(jnp.cumsum(one_hot, axis=0) * one_hot, axis=1) - 1
    code = owners * capacity + rank
    meta = jnp.concatenate([segment_ids[0], code, chosen % EXP_DEV]).astype(jnp.bfloat16)
    meta_w = feat + HEAD_DIM
    meta_rows = -(-meta.shape[0] // meta_w)
    meta = jnp.pad(meta, (0, meta_rows * meta_w - meta.shape[0])).reshape(meta_rows, meta_w)
    payload = jnp.concatenate(
        [
            jnp.concatenate([q_send, kv_send], axis=2),
            jnp.broadcast_to(meta[None, :, :], (n_seq, meta_rows, meta_w)),
        ],
        axis=1,
    )
    got_in = lax.all_to_all(payload, "seq", split_axis=0, concat_axis=0, tiled=True)
    got_in = got_in.reshape(n_seq, tok_rows + meta_rows, meta_w)
    q_all = got_in[:, :tok_rows, :feat].reshape(length, heads_here, HEAD_DIM)
    kv_mine = got_in[:, :tok_rows, feat:].reshape(n_seq, half, 2 * HEAD_DIM)
    kv_other = lax.ppermute(kv_mine, "seq", [(i, i ^ 1) for i in range(n_seq)])
    even = lax.axis_index("seq") % 2 == 0
    kv_all = jnp.stack(
        [jnp.where(even, kv_mine, kv_other), jnp.where(even, kv_other, kv_mine)], axis=1
    ).reshape(length, 2 * HEAD_DIM)
    k_all = kv_all[:, :HEAD_DIM]
    v_all = kv_all[:, HEAD_DIM:]
    meta_all = got_in[:, tok_rows:, :].reshape(n_seq, meta_rows * meta_w)[:, : 3 * tok_rows]
    meta_all = meta_all.astype(jnp.int32)
    segments = meta_all[:, :tok_rows].reshape(length)
    code_all = meta_all[:, tok_rows : 2 * tok_rows]
    adapter_all = meta_all[:, 2 * tok_rows :]

    context = attend(q_all, k_all, v_all, segments).reshape(length, feat)

    pick = code_all[:, None, :] == jnp.arange(devices * capacity, dtype=jnp.int32)[None, :, None]
    pick = pick.astype(jnp.bfloat16)
    send = jnp.einsum(
        "jmt,jtf->mjf",
        pick,
        context.reshape(n_seq, tok_rows, feat),
        preferred_element_type=jnp.float32,
    ).astype(jnp.bfloat16)
    send = send.reshape(devices, slots, feat)
    tags = jnp.einsum(
        "jmt,jt->mj",
        pick,
        (adapter_all.reshape(n_seq, tok_rows) + 1).astype(jnp.bfloat16),
        preferred_element_type=jnp.float32,
    ).reshape(devices, slots) - 1.0
    tag_row = jnp.pad(tags.astype(jnp.bfloat16), ((0, 0), (0, feat - slots)))
    send = jnp.concatenate([send, tag_row[:, None, :]], axis=1)
    got = lax.all_to_all(send, ("seq", "store"), split_axis=0, concat_axis=0, tiled=True)
    got = got.reshape(n_seq, n_store, slots + 1, feat)
    rows = jnp.transpose(
        got[:, :, :slots, :].reshape(n_seq, n_store, capacity, n_seq, feat), (3, 1, 2, 0, 4)
    ).reshape(n_store * slots, width)
    row_tags = jnp.transpose(
        got[0, :, slots, :slots].reshape(n_store, capacity, n_seq), (2, 0, 1)
    ).reshape(n_store * slots, 1).astype(jnp.float32)

    low = jnp.dot(rows, adapter_down, preferred_element_type=jnp.float32)
    lane_owner = (jnp.arange(low.shape[1], dtype=jnp.int32) // RANK).astype(jnp.float32)
    low = jnp.where(row_tags == lane_owner[None, :], low, 0.0).astype(jnp.bfloat16)
    delta = jnp.dot(low, adapter_up, preferred_element_type=jnp.float32).astype(jnp.bfloat16)
    mixed_rows = (rows.astype(jnp.float32) + delta.astype(jnp.float32)).astype(jnp.bfloat16)
    ret = mixed_rows.reshape(devices, capacity, width)
    back = lax.all_to_all(ret, ("seq", "store"), split_axis=0, concat_axis=0, tiled=True)
    mixed = back[owners, rank]
    return mixed[None]


def solution(mesh):
    return jax.shard_map(
        local,
        mesh=mesh,
        in_specs=(
            P("store", "seq", None),
            P("store", "seq", None),
            P("store", "seq", None),
            P("store", "seq"),
            P("store", "seq"),
            P(None, ("seq", "store")),
            P(("seq", "store"), None),
        ),
        out_specs=P("store", "seq", None),
        check_vma=False,
    )
```

```python
import functools

import jax
import jax.numpy as jnp
from jax import lax
from jax.experimental import pallas as pl
from jax.experimental.pallas import tpu as pltpu
from jax.sharding import PartitionSpec as P

HEAD_DIM = 128
HEADS = 32
KV_HEADS = 4
RANK = 64
EXP_DEV = 16
MAX_DOC = 2048
N_DOCS = 4


def _attn_kernel(lo_ref, full_ref, bnd_ref, q_ref, kt_ref, v_ref, o_ref, s_ref, *, bq, bk, scale):
    i = pl.program_id(0)
    lanes = 128
    nb = s_ref.shape[0]
    lo = jnp.maximum(lo_ref[i], i - (nb - 1))
    mid = jnp.clip(full_ref[i], lo, i)
    q = q_ref[...]
    qpos = i * bq + lax.broadcasted_iota(jnp.int32, (bq, 1), 0)
    qs = jnp.zeros((bq, 1), jnp.int32)
    for c in range(N_DOCS - 1):
        qs = jnp.where(qpos >= bnd_ref[c], bnd_ref[c], qs)

    def raw(kb):
        start = pl.multiple_of(kb * bk, bk)
        s = jnp.dot(q, kt_ref[:, pl.ds(start, bk)], preferred_element_type=jnp.float32)
        return s * scale, start

    def masked(kb):
        s, start = raw(kb)
        kpos = start + lax.broadcasted_iota(jnp.int32, (1, bk), 1)
        ok = (kpos >= qs) & (kpos <= qpos)
        return jnp.where(ok, s, jnp.float32(-1e30)), start

    def keep(kb, m, s):
        s_ref[kb - lo] = s
        for c in range(bk // lanes):
            m = jnp.maximum(m, s[:, c * lanes : (c + 1) * lanes])
        return m

    m = jnp.full((bq, lanes), -1e30, jnp.float32)
    m = lax.fori_loop(lo, mid, lambda kb, m: keep(kb, m, masked(kb)[0]), m)
    m = lax.fori_loop(mid, i, lambda kb, m: keep(kb, m, raw(kb)[0]), m)
    m = keep(i, m, masked(i)[0])
    top = jnp.max(m, axis=1, keepdims=True)

    def accum(kb, carry):
        tot, acc = carry
        p = jnp.exp(s_ref[kb - lo] - top)
        for c in range(bk // lanes):
            tot = tot + p[:, c * lanes : (c + 1) * lanes]
        v = v_ref[pl.ds(pl.multiple_of(kb * bk, bk), bk), :]
        acc = acc + jnp.dot(p.astype(jnp.bfloat16), v, preferred_element_type=jnp.float32)
        return tot, acc

    carry = (jnp.zeros((bq, lanes), jnp.float32), jnp.zeros((bq, q.shape[1]), jnp.float32))
    tot, acc = lax.fori_loop(lo, i + 1, accum, carry)
    total = jnp.sum(tot, axis=1, keepdims=True)
    o_ref[...] = (acc / total).astype(o_ref.dtype)


def attend(queries, key_rows, value_rows, segments):
    length, dim = key_rows.shape
    bq = min(512, length)
    bk = min(512, length)
    n_q = length // bq
    bounds = jnp.sum(
        segments[None, :] < jnp.arange(1, N_DOCS, dtype=jnp.int32)[:, None], axis=1
    ).astype(jnp.int32)

    def doc_start_at(t):
        first = jnp.zeros_like(t)
        for c in range(N_DOCS - 1):
            first = jnp.where(t >= bounds[c], bounds[c], first)
        return first

    firsts = jnp.arange(n_q, dtype=jnp.int32) * bq
    lo_blk = doc_start_at(firsts) // bk
    full_blk = (doc_start_at(firsts + bq - 1) + bk - 1) // bk
    q_rows = queries.reshape(length, dim)
    kernel = functools.partial(_attn_kernel, bq=bq, bk=bk, scale=dim ** (-0.5))
    band = (MAX_DOC + bq - 1) // bk + 1
    out = pl.pallas_call(
        kernel,
        out_shape=jax.ShapeDtypeStruct((length, dim), jnp.bfloat16),
        grid_spec=pltpu.PrefetchScalarGridSpec(
            num_scalar_prefetch=3,
            grid=(n_q,),
            in_specs=[
                pl.BlockSpec((bq, dim), lambda i, lo, full, bnd: (i, 0)),
                pl.BlockSpec((dim, length), lambda i, lo, full, bnd: (0, 0)),
                pl.BlockSpec((length, dim), lambda i, lo, full, bnd: (0, 0)),
            ],
            out_specs=pl.BlockSpec((bq, dim), lambda i, lo, full, bnd: (i, 0)),
            scratch_shapes=[pltpu.VMEM((min(band, n_q), bq, bk), jnp.float32)],
        ),
        compiler_params=pltpu.CompilerParams(vmem_limit_bytes=48 * 1024 * 1024),
        cost_estimate=pl.CostEstimate(
            flops=6 * length * MAX_DOC * dim,
            transcendentals=length * MAX_DOC,
            bytes_accessed=8 * length * dim,
        ),
    )(lo_blk, full_blk, bounds, q_rows, key_rows.T, value_rows)
    return out


def local(queries, keys, values, segment_ids, route_ids, adapter_down, adapter_up):
    n_seq = lax.axis_size("seq")
    n_store = lax.axis_size("store")
    tok_rows = queries.shape[1]
    width = queries.shape[2]
    length = tok_rows * n_seq
    heads_here = HEADS // n_seq
    feat = heads_here * HEAD_DIM
    group = HEADS // KV_HEADS
    devices = n_seq * n_store
    capacity = max(2, 2 * tok_rows // devices)
    slots = n_seq * capacity

    half = tok_rows // 2
    q_send = queries[0].reshape(tok_rows, n_seq, feat)
    paired = jnp.concatenate(
        [keys[0].reshape(tok_rows, KV_HEADS, HEAD_DIM), values[0].reshape(tok_rows, KV_HEADS, HEAD_DIM)],
        axis=2,
    )
    halves = jnp.transpose(paired.reshape(2, half, KV_HEADS, 2 * HEAD_DIM), (0, 2, 1, 3)).reshape(
        2 * KV_HEADS, half, 2 * HEAD_DIM
    )
    dest = jnp.arange(n_seq, dtype=jnp.int32)
    kv_send = jnp.take(halves, (dest % 2) * KV_HEADS + (dest * heads_here) // group, axis=0)
    kv_send = jnp.transpose(kv_send.reshape(n_seq, tok_rows, HEAD_DIM), (1, 0, 2))
    chosen = route_ids[0]
    owners = chosen // EXP_DEV
    one_hot = (owners[:, None] == jnp.arange(devices, dtype=jnp.int32)[None, :]).astype(jnp.int32)
    rank = jnp.sum(jnp.cumsum(one_hot, axis=0) * one_hot, axis=1) - 1
    code = owners * capacity + rank
    meta = jnp.concatenate([segment_ids[0], code, chosen % EXP_DEV]).astype(jnp.bfloat16)
    meta_w = feat + HEAD_DIM
    meta_rows = -(-meta.shape[0] // meta_w)
    meta = jnp.pad(meta, (0, meta_rows * meta_w - meta.shape[0])).reshape(meta_rows, meta_w)
    payload = jnp.concatenate(
        [
            jnp.concatenate([q_send, kv_send], axis=2),
            jnp.broadcast_to(meta[:, None, :], (meta_rows, n_seq, meta_w)),
        ],
        axis=0,
    )
    got_in = lax.all_to_all(payload, "seq", split_axis=1, concat_axis=0, tiled=True)
    got_in = got_in.reshape(n_seq, tok_rows + meta_rows, meta_w)
    q_all = got_in[:, :tok_rows, :feat].reshape(length, heads_here, HEAD_DIM)
    kv_mine = got_in[:, :tok_rows, feat:].reshape(n_seq, half, 2 * HEAD_DIM)
    kv_other = lax.ppermute(kv_mine, "seq", [(i, i ^ 1) for i in range(n_seq)])
    even = lax.axis_index("seq") % 2 == 0
    kv_all = jnp.stack(
        [jnp.where(even, kv_mine, kv_other), jnp.where(even, kv_other, kv_mine)], axis=1
    ).reshape(length, 2 * HEAD_DIM)
    k_all = kv_all[:, :HEAD_DIM]
    v_all = kv_all[:, HEAD_DIM:]
    meta_all = got_in[:, tok_rows:, :].reshape(n_seq, meta_rows * meta_w)[:, : 3 * tok_rows]
    meta_all = meta_all.astype(jnp.int32)
    segments = meta_all[:, :tok_rows].reshape(length)
    code_all = meta_all[:, tok_rows : 2 * tok_rows]
    adapter_all = meta_all[:, 2 * tok_rows :]

    context = attend(q_all, k_all, v_all, segments).reshape(length, feat)

    pick = code_all[:, None, :] == jnp.arange(devices * capacity, dtype=jnp.int32)[None, :, None]
    pick = pick.astype(jnp.bfloat16)
    send = jnp.einsum(
        "jmt,jtf->jmf",
        pick,
        context.reshape(n_seq, tok_rows, feat),
        preferred_element_type=jnp.float32,
    ).astype(jnp.bfloat16)
    send = send.reshape(n_seq, devices, capacity, feat)
    tags = jnp.einsum(
        "jmt,jt->mj",
        pick,
        (adapter_all.reshape(n_seq, tok_rows) + 1).astype(jnp.bfloat16),
        preferred_element_type=jnp.float32,
    ).reshape(devices, capacity, n_seq) - 1.0
    tag_plane = jnp.pad(tags.astype(jnp.bfloat16), ((0, 0), (0, 0), (0, feat - n_seq)))
    send = jnp.concatenate([send, tag_plane[None]], axis=0)
    got = lax.all_to_all(send, ("seq", "store"), split_axis=1, concat_axis=1, tiled=True)
    rows = jnp.transpose(
        got[:n_seq].reshape(n_seq, n_seq, n_store, capacity, feat), (0, 2, 3, 1, 4)
    ).reshape(n_store * slots, width)
    row_tags = jnp.transpose(got[n_seq, :n_store, :, :n_seq], (2, 0, 1)).reshape(
        n_store * slots, 1
    ).astype(jnp.float32)

    low = jnp.dot(rows, adapter_down, preferred_element_type=jnp.float32)
    lane_owner = (jnp.arange(low.shape[1], dtype=jnp.int32) // RANK).astype(jnp.float32)
    low = jnp.where(row_tags == lane_owner[None, :], low, 0.0).astype(jnp.bfloat16)
    delta = jnp.dot(low, adapter_up, preferred_element_type=jnp.float32).astype(jnp.bfloat16)
    mixed_rows = (rows.astype(jnp.float32) + delta.astype(jnp.float32)).astype(jnp.bfloat16)
    ret = mixed_rows.reshape(devices, capacity, width)
    back = lax.all_to_all(ret, ("seq", "store"), split_axis=0, concat_axis=0, tiled=True)
    mixed = back[owners, rank]
    return mixed[None]


def solution(mesh):
    return jax.shard_map(
        local,
        mesh=mesh,
        in_specs=(
            P("store", "seq", None),
            P("store", "seq", None),
            P("store", "seq", None),
            P("store", "seq"),
            P("store", "seq"),
            P(None, ("seq", "store")),
            P(("seq", "store"), None),
        ),
        out_specs=P("store", "seq", None),
        check_vma=False,
    )
```

```python
import functools

import jax
import jax.numpy as jnp
from jax import lax
from jax.experimental import pallas as pl
from jax.experimental.pallas import tpu as pltpu
from jax.sharding import PartitionSpec as P

HEAD_DIM = 128
HEADS = 32
KV_HEADS = 4
RANK = 64
EXP_DEV = 16
MAX_DOC = 2048
N_DOCS = 4


def _attn_kernel(lo_ref, full_ref, bnd_ref, q_ref, kt_ref, v_ref, o_ref, s_ref, *, bq, bk, scale):
    i = pl.program_id(0)
    lanes = 128
    nb = s_ref.shape[0]
    lo = jnp.maximum(lo_ref[i], i - (nb - 1))
    mid = jnp.clip(full_ref[i], lo, i)
    q = q_ref[...]
    qpos = i * bq + lax.broadcasted_iota(jnp.int32, (bq, 1), 0)
    qs = jnp.zeros((bq, 1), jnp.int32)
    for c in range(N_DOCS - 1):
        qs = jnp.where(qpos >= bnd_ref[c], bnd_ref[c], qs)

    def raw(kb):
        start = pl.multiple_of(kb * bk, bk)
        s = jnp.dot(q, kt_ref[:, pl.ds(start, bk)], preferred_element_type=jnp.float32)
        return s * scale, start

    def masked(kb):
        s, start = raw(kb)
        kpos = start + lax.broadcasted_iota(jnp.int32, (1, bk), 1)
        ok = (kpos >= qs) & (kpos <= qpos)
        return jnp.where(ok, s, jnp.float32(-1e30)), start

    def keep(kb, m, s):
        s_ref[kb - lo] = s
        for c in range(bk // lanes):
            m = jnp.maximum(m, s[:, c * lanes : (c + 1) * lanes])
        return m

    m = jnp.full((bq, lanes), -1e30, jnp.float32)
    m = lax.fori_loop(lo, mid, lambda kb, m: keep(kb, m, masked(kb)[0]), m)
    m = lax.fori_loop(mid, i, lambda kb, m: keep(kb, m, raw(kb)[0]), m)
    m = keep(i, m, masked(i)[0])
    top = jnp.max(m, axis=1, keepdims=True)

    def accum(kb, carry):
        tot, acc = carry
        p = jnp.exp(s_ref[kb - lo] - top)
        for c in range(bk // lanes):
            tot = tot + p[:, c * lanes : (c + 1) * lanes]
        v = v_ref[pl.ds(pl.multiple_of(kb * bk, bk), bk), :]
        acc = acc + jnp.dot(p.astype(jnp.bfloat16), v, preferred_element_type=jnp.float32)
        return tot, acc

    carry = (jnp.zeros((bq, lanes), jnp.float32), jnp.zeros((bq, q.shape[1]), jnp.float32))
    tot, acc = lax.fori_loop(lo, i + 1, accum, carry)
    total = jnp.sum(tot, axis=1, keepdims=True)
    o_ref[...] = (acc / total).astype(o_ref.dtype)


def attend(queries, key_rows, value_rows, segments):
    length, dim = key_rows.shape
    bq = min(512, length)
    bk = min(512, length)
    n_q = length // bq
    bounds = jnp.sum(
        segments[None, :] < jnp.arange(1, N_DOCS, dtype=jnp.int32)[:, None], axis=1
    ).astype(jnp.int32)

    def doc_start_at(t):
        first = jnp.zeros_like(t)
        for c in range(N_DOCS - 1):
            first = jnp.where(t >= bounds[c], bounds[c], first)
        return first

    firsts = jnp.arange(n_q, dtype=jnp.int32) * bq
    lo_blk = doc_start_at(firsts) // bk
    full_blk = (doc_start_at(firsts + bq - 1) + bk - 1) // bk
    q_rows = queries.reshape(length, dim)
    kernel = functools.partial(_attn_kernel, bq=bq, bk=bk, scale=dim ** (-0.5))
    band = (MAX_DOC + bq - 1) // bk + 1
    out = pl.pallas_call(
        kernel,
        out_shape=jax.ShapeDtypeStruct((length, dim), jnp.bfloat16),
        grid_spec=pltpu.PrefetchScalarGridSpec(
            num_scalar_prefetch=3,
            grid=(n_q,),
            in_specs=[
                pl.BlockSpec((bq, dim), lambda i, lo, full, bnd: (i, 0)),
                pl.BlockSpec((dim, length), lambda i, lo, full, bnd: (0, 0)),
                pl.BlockSpec((length, dim), lambda i, lo, full, bnd: (0, 0)),
            ],
            out_specs=pl.BlockSpec((bq, dim), lambda i, lo, full, bnd: (i, 0)),
            scratch_shapes=[pltpu.VMEM((min(band, n_q), bq, bk), jnp.float32)],
        ),
        compiler_params=pltpu.CompilerParams(vmem_limit_bytes=48 * 1024 * 1024),
        cost_estimate=pl.CostEstimate(
            flops=6 * length * MAX_DOC * dim,
            transcendentals=length * MAX_DOC,
            bytes_accessed=8 * length * dim,
        ),
    )(lo_blk, full_blk, bounds, q_rows, key_rows.T, value_rows)
    return out


def local(queries, keys, values, segment_ids, route_ids, adapter_down, adapter_up):
    n_seq = lax.axis_size("seq")
    n_store = lax.axis_size("store")
    tok_rows = queries.shape[1]
    width = queries.shape[2]
    length = tok_rows * n_seq
    heads_here = HEADS // n_seq
    feat = heads_here * HEAD_DIM
    group = HEADS // KV_HEADS
    devices = n_seq * n_store
    capacity = max(2, 2 * tok_rows // devices)
    slots = n_seq * capacity

    half = tok_rows // 2
    q_send = queries[0].reshape(tok_rows, n_seq, feat)
    paired = jnp.concatenate(
        [keys[0].reshape(tok_rows, KV_HEADS, HEAD_DIM), values[0].reshape(tok_rows, KV_HEADS, HEAD_DIM)],
        axis=2,
    )
    halves = jnp.transpose(paired.reshape(2, half, KV_HEADS, 2 * HEAD_DIM), (0, 2, 1, 3)).reshape(
        2 * KV_HEADS, half, 2 * HEAD_DIM
    )
    if heads_here == 1 and group % 2 == 0 and n_seq == KV_HEADS * group:
        kv_send = jnp.broadcast_to(
            jnp.transpose(halves.reshape(2, KV_HEADS, half, 2 * HEAD_DIM), (1, 0, 2, 3))[:, None],
            (KV_HEADS, group // 2, 2, half, 2 * HEAD_DIM),
        ).reshape(n_seq, half, 2 * HEAD_DIM)
    else:
        dest = jnp.arange(n_seq, dtype=jnp.int32)
        kv_send = jnp.take(halves, (dest % 2) * KV_HEADS + (dest * heads_here) // group, axis=0)
    kv_send = jnp.transpose(kv_send.reshape(n_seq, tok_rows, HEAD_DIM), (1, 0, 2))
    chosen = route_ids[0]
    owners = chosen // EXP_DEV
    one_hot = (owners[:, None] == jnp.arange(devices, dtype=jnp.int32)[None, :]).astype(jnp.int32)
    rank = jnp.sum(jnp.cumsum(one_hot, axis=0) * one_hot, axis=1) - 1
    code = owners * capacity + rank
    meta = jnp.concatenate([segment_ids[0], code, chosen % EXP_DEV]).astype(jnp.bfloat16)
    meta_w = feat + HEAD_DIM
    meta_rows = -(-meta.shape[0] // meta_w)
    meta = jnp.pad(meta, (0, meta_rows * meta_w - meta.shape[0])).reshape(meta_rows, meta_w)
    payload = jnp.concatenate(
        [
            jnp.concatenate([q_send, kv_send], axis=2),
            jnp.broadcast_to(meta[:, None, :], (meta_rows, n_seq, meta_w)),
        ],
        axis=0,
    )
    got_in = lax.all_to_all(payload, "seq", split_axis=1, concat_axis=0, tiled=True)
    got_in = got_in.reshape(n_seq, tok_rows + meta_rows, meta_w)
    q_all = got_in[:, :tok_rows, :feat].reshape(length, heads_here, HEAD_DIM)
    kv_mine = got_in[:, :tok_rows, feat:].reshape(n_seq, half, 2 * HEAD_DIM)
    kv_other = lax.ppermute(kv_mine, "seq", [(i, i ^ 1) for i in range(n_seq)])
    even = lax.axis_index("seq") % 2 == 0
    kv_all = jnp.stack(
        [jnp.where(even, kv_mine, kv_other), jnp.where(even, kv_other, kv_mine)], axis=1
    ).reshape(length, 2 * HEAD_DIM)
    k_all = kv_all[:, :HEAD_DIM]
    v_all = kv_all[:, HEAD_DIM:]
    meta_all = got_in[:, tok_rows:, :].reshape(n_seq, meta_rows * meta_w)[:, : 3 * tok_rows]
    meta_all = meta_all.astype(jnp.int32)
    segments = meta_all[:, :tok_rows].reshape(length)
    code_all = meta_all[:, tok_rows : 2 * tok_rows]
    adapter_all = meta_all[:, 2 * tok_rows :]

    context = attend(q_all, k_all, v_all, segments).reshape(length, feat)

    pick = code_all[:, None, :] == jnp.arange(devices * capacity, dtype=jnp.int32)[None, :, None]
    pick = pick.astype(jnp.bfloat16)
    send = jnp.einsum(
        "jmt,jtf->mjf",
        pick,
        context.reshape(n_seq, tok_rows, feat),
        preferred_element_type=jnp.float32,
    ).astype(jnp.bfloat16)
    send = send.reshape(devices, slots, feat)
    tags = jnp.einsum(
        "jmt,jt->mj",
        pick,
        (adapter_all.reshape(n_seq, tok_rows) + 1).astype(jnp.bfloat16),
        preferred_element_type=jnp.float32,
    ).reshape(devices, slots) - 1.0
    tag_row = jnp.pad(tags.astype(jnp.bfloat16), ((0, 0), (0, feat - slots)))
    send = jnp.concatenate([send, tag_row[:, None, :]], axis=1)
    got = lax.all_to_all(send, ("seq", "store"), split_axis=0, concat_axis=0, tiled=True)
    got = got.reshape(n_seq, n_store, slots + 1, feat)
    rows = jnp.transpose(
        got[:, :, :slots, :].reshape(n_seq, n_store, capacity, n_seq, feat), (3, 1, 2, 0, 4)
    ).reshape(n_store * slots, width)
    row_tags = jnp.transpose(
        got[0, :, slots, :slots].reshape(n_store, capacity, n_seq), (2, 0, 1)
    ).reshape(n_store * slots, 1).astype(jnp.float32)

    low = jnp.dot(rows, adapter_down, preferred_element_type=jnp.float32)
    lane_owner = (jnp.arange(low.shape[1], dtype=jnp.int32) // RANK).astype(jnp.float32)
    low = jnp.where(row_tags == lane_owner[None, :], low, 0.0).astype(jnp.bfloat16)
    delta = jnp.dot(low, adapter_up, preferred_element_type=jnp.float32).astype(jnp.bfloat16)
    mixed_rows = (rows.astype(jnp.float32) + delta.astype(jnp.float32)).astype(jnp.bfloat16)
    ret = mixed_rows.reshape(devices, capacity, width)
    back = lax.all_to_all(ret, ("seq", "store"), split_axis=0, concat_axis=0, tiled=True)
    mixed = back[owners, rank]
    return mixed[None]


def solution(mesh):
    return jax.shard_map(
        local,
        mesh=mesh,
        in_specs=(
            P("store", "seq", None),
            P("store", "seq", None),
            P("store", "seq", None),
            P("store", "seq"),
            P("store", "seq"),
            P(None, ("seq", "store")),
            P(("seq", "store"), None),
        ),
        out_specs=P("store", "seq", None),
        check_vma=False,
    )
```

```python
import functools

import jax
import jax.numpy as jnp
from jax import lax
from jax.experimental import pallas as pl
from jax.experimental.pallas import tpu as pltpu
from jax.sharding import PartitionSpec as P

HEAD_DIM = 128
HEADS = 32
KV_HEADS = 4
RANK = 64
EXP_DEV = 16
MAX_DOC = 2048
N_DOCS = 4


def _attn_kernel(lo_ref, full_ref, bnd_ref, q_ref, kt_ref, v_ref, o_ref, s_ref, *, bq, bk, scale):
    i = pl.program_id(0)
    lanes = 128
    nb = s_ref.shape[0]
    lo = jnp.maximum(lo_ref[i], i - (nb - 1))
    mid = jnp.clip(full_ref[i], lo, i)
    q = q_ref[...]
    qpos = i * bq + lax.broadcasted_iota(jnp.int32, (bq, 1), 0)
    qs = jnp.zeros((bq, 1), jnp.int32)
    for c in range(N_DOCS - 1):
        qs = jnp.where(qpos >= bnd_ref[c], bnd_ref[c], qs)

    def raw(kb):
        start = pl.multiple_of(kb * bk, bk)
        s = jnp.dot(q, kt_ref[:, pl.ds(start, bk)], preferred_element_type=jnp.float32)
        return s * scale, start

    def masked(kb):
        s, start = raw(kb)
        kpos = start + lax.broadcasted_iota(jnp.int32, (1, bk), 1)
        ok = (kpos >= qs) & (kpos <= qpos)
        return jnp.where(ok, s, jnp.float32(-1e30)), start

    def keep(kb, m, s):
        s_ref[kb - lo] = s
        for c in range(bk // lanes):
            m = jnp.maximum(m, s[:, c * lanes : (c + 1) * lanes])
        return m

    m = jnp.full((bq, lanes), -1e30, jnp.float32)
    m = lax.fori_loop(lo, mid, lambda kb, m: keep(kb, m, masked(kb)[0]), m)
    m = lax.fori_loop(mid, i, lambda kb, m: keep(kb, m, raw(kb)[0]), m)
    m = keep(i, m, masked(i)[0])
    top = jnp.max(m, axis=1, keepdims=True)

    def accum(kb, carry):
        tot, acc = carry
        p = jnp.exp(s_ref[kb - lo] - top)
        for c in range(bk // lanes):
            tot = tot + p[:, c * lanes : (c + 1) * lanes]
        v = v_ref[pl.ds(pl.multiple_of(kb * bk, bk), bk), :]
        acc = acc + jnp.dot(p.astype(jnp.bfloat16), v, preferred_element_type=jnp.float32)
        return tot, acc

    carry = (jnp.zeros((bq, lanes), jnp.float32), jnp.zeros((bq, q.shape[1]), jnp.float32))
    tot, acc = lax.fori_loop(lo, i + 1, accum, carry)
    total = jnp.sum(tot, axis=1, keepdims=True)
    o_ref[...] = (acc / total).astype(o_ref.dtype)


def attend(queries, key_rows, value_rows, segments):
    length, dim = key_rows.shape
    bq = min(1024, length)
    bk = min(1024, length)
    n_q = length // bq
    bounds = jnp.sum(
        segments[None, :] < jnp.arange(1, N_DOCS, dtype=jnp.int32)[:, None], axis=1
    ).astype(jnp.int32)

    def doc_start_at(t):
        first = jnp.zeros_like(t)
        for c in range(N_DOCS - 1):
            first = jnp.where(t >= bounds[c], bounds[c], first)
        return first

    firsts = jnp.arange(n_q, dtype=jnp.int32) * bq
    lo_blk = doc_start_at(firsts) // bk
    full_blk = (doc_start_at(firsts + bq - 1) + bk - 1) // bk
    q_rows = queries.reshape(length, dim)
    kernel = functools.partial(_attn_kernel, bq=bq, bk=bk, scale=dim ** (-0.5))
    band = (MAX_DOC + bq - 1) // bk + 1
    out = pl.pallas_call(
        kernel,
        out_shape=jax.ShapeDtypeStruct((length, dim), jnp.bfloat16),
        grid_spec=pltpu.PrefetchScalarGridSpec(
            num_scalar_prefetch=3,
            grid=(n_q,),
            in_specs=[
                pl.BlockSpec((bq, dim), lambda i, lo, full, bnd: (i, 0)),
                pl.BlockSpec((dim, length), lambda i, lo, full, bnd: (0, 0)),
                pl.BlockSpec((length, dim), lambda i, lo, full, bnd: (0, 0)),
            ],
            out_specs=pl.BlockSpec((bq, dim), lambda i, lo, full, bnd: (i, 0)),
            scratch_shapes=[pltpu.VMEM((min(band, n_q), bq, bk), jnp.float32)],
        ),
        compiler_params=pltpu.CompilerParams(vmem_limit_bytes=48 * 1024 * 1024),
        cost_estimate=pl.CostEstimate(
            flops=6 * length * MAX_DOC * dim,
            transcendentals=length * MAX_DOC,
            bytes_accessed=8 * length * dim,
        ),
    )(lo_blk, full_blk, bounds, q_rows, key_rows.T, value_rows)
    return out


def local(queries, keys, values, segment_ids, route_ids, adapter_down, adapter_up):
    n_seq = lax.axis_size("seq")
    n_store = lax.axis_size("store")
    tok_rows = queries.shape[1]
    width = queries.shape[2]
    length = tok_rows * n_seq
    heads_here = HEADS // n_seq
    feat = heads_here * HEAD_DIM
    group = HEADS // KV_HEADS
    devices = n_seq * n_store
    capacity = max(2, 2 * tok_rows // devices)
    slots = n_seq * capacity

    half = tok_rows // 2
    q_send = queries[0].reshape(tok_rows, n_seq, feat)
    paired = jnp.concatenate(
        [keys[0].reshape(tok_rows, KV_HEADS, HEAD_DIM), values[0].reshape(tok_rows, KV_HEADS, HEAD_DIM)],
        axis=2,
    )
    halves = jnp.transpose(paired.reshape(2, half, KV_HEADS, 2 * HEAD_DIM), (0, 2, 1, 3)).reshape(
        2 * KV_HEADS, half, 2 * HEAD_DIM
    )
    dest = jnp.arange(n_seq, dtype=jnp.int32)
    kv_send = jnp.take(halves, (dest % 2) * KV_HEADS + (dest * heads_here) // group, axis=0)
    kv_send = jnp.transpose(kv_send.reshape(n_seq, tok_rows, HEAD_DIM), (1, 0, 2))
    chosen = route_ids[0]
    owners = chosen // EXP_DEV
    one_hot = (owners[:, None] == jnp.arange(devices, dtype=jnp.int32)[None, :]).astype(jnp.int32)
    rank = jnp.sum(jnp.cumsum(one_hot, axis=0) * one_hot, axis=1) - 1
    code = owners * capacity + rank
    meta = jnp.concatenate([segment_ids[0], code, chosen % EXP_DEV]).astype(jnp.bfloat16)
    meta_w = feat + HEAD_DIM
    meta_rows = -(-meta.shape[0] // meta_w)
    meta = jnp.pad(meta, (0, meta_rows * meta_w - meta.shape[0])).reshape(meta_rows, meta_w)
    payload = jnp.concatenate(
        [
            jnp.concatenate([q_send, kv_send], axis=2),
            jnp.broadcast_to(meta[:, None, :], (meta_rows, n_seq, meta_w)),
        ],
        axis=0,
    )
    got_in = lax.all_to_all(payload, "seq", split_axis=1, concat_axis=0, tiled=True)
    got_in = got_in.reshape(n_seq, tok_rows + meta_rows, meta_w)
    q_all = got_in[:, :tok_rows, :feat].reshape(length, heads_here, HEAD_DIM)
    kv_mine = got_in[:, :tok_rows, feat:].reshape(n_seq, half, 2 * HEAD_DIM)
    kv_other = lax.ppermute(kv_mine, "seq", [(i, i ^ 1) for i in range(n_seq)])
    even = lax.axis_index("seq") % 2 == 0
    kv_all = jnp.stack(
        [jnp.where(even, kv_mine, kv_other), jnp.where(even, kv_other, kv_mine)], axis=1
    ).reshape(length, 2 * HEAD_DIM)
    k_all = kv_all[:, :HEAD_DIM]
    v_all = kv_all[:, HEAD_DIM:]
    meta_all = got_in[:, tok_rows:, :].reshape(n_seq, meta_rows * meta_w)[:, : 3 * tok_rows]
    meta_all = meta_all.astype(jnp.int32)
    segments = meta_all[:, :tok_rows].reshape(length)
    code_all = meta_all[:, tok_rows : 2 * tok_rows]
    adapter_all = meta_all[:, 2 * tok_rows :]

    context = attend(q_all, k_all, v_all, segments).reshape(length, feat)

    pick = code_all[:, None, :] == jnp.arange(devices * capacity, dtype=jnp.int32)[None, :, None]
    pick = pick.astype(jnp.bfloat16)
    send = jnp.einsum(
        "jmt,jtf->mjf",
        pick,
        context.reshape(n_seq, tok_rows, feat),
        preferred_element_type=jnp.float32,
    ).astype(jnp.bfloat16)
    send = send.reshape(devices, slots, feat)
    tags = jnp.einsum(
        "jmt,jt->mj",
        pick,
        (adapter_all.reshape(n_seq, tok_rows) + 1).astype(jnp.bfloat16),
        preferred_element_type=jnp.float32,
    ).reshape(devices, slots) - 1.0
    tag_row = jnp.pad(tags.astype(jnp.bfloat16), ((0, 0), (0, feat - slots)))
    send = jnp.concatenate([send, tag_row[:, None, :]], axis=1)
    got = lax.all_to_all(send, ("seq", "store"), split_axis=0, concat_axis=0, tiled=True)
    got = got.reshape(n_seq, n_store, slots + 1, feat)
    rows = jnp.transpose(
        got[:, :, :slots, :].reshape(n_seq, n_store, capacity, n_seq, feat), (3, 1, 2, 0, 4)
    ).reshape(n_store * slots, width)
    row_tags = jnp.transpose(
        got[0, :, slots, :slots].reshape(n_store, capacity, n_seq), (2, 0, 1)
    ).reshape(n_store * slots, 1).astype(jnp.float32)

    low = jnp.dot(rows, adapter_down, preferred_element_type=jnp.float32)
    lane_owner = (jnp.arange(low.shape[1], dtype=jnp.int32) // RANK).astype(jnp.float32)
    low = jnp.where(row_tags == lane_owner[None, :], low, 0.0).astype(jnp.bfloat16)
    delta = jnp.dot(low, adapter_up, preferred_element_type=jnp.float32).astype(jnp.bfloat16)
    mixed_rows = (rows.astype(jnp.float32) + delta.astype(jnp.float32)).astype(jnp.bfloat16)
    ret = mixed_rows.reshape(devices, capacity, width)
    back = lax.all_to_all(ret, ("seq", "store"), split_axis=0, concat_axis=0, tiled=True)
    mixed = back[owners, rank]
    return mixed[None]


def solution(mesh):
    return jax.shard_map(
        local,
        mesh=mesh,
        in_specs=(
            P("store", "seq", None),
            P("store", "seq", None),
            P("store", "seq", None),
            P("store", "seq"),
            P("store", "seq"),
            P(None, ("seq", "store")),
            P(("seq", "store"), None),
        ),
        out_specs=P("store", "seq", None),
        check_vma=False,
    )
```

```python
import functools

import jax
import jax.numpy as jnp
from jax import lax
from jax.experimental import pallas as pl
from jax.experimental.pallas import tpu as pltpu
from jax.sharding import PartitionSpec as P

HEAD_DIM = 128
HEADS = 32
KV_HEADS = 4
RANK = 64
EXP_DEV = 16
MAX_DOC = 2048
N_DOCS = 4


def _attn_kernel(lo_ref, full_ref, bnd_ref, q_ref, kt_ref, v_ref, o_ref, s_ref, *, bq, bk, scale):
    i = pl.program_id(0)
    lanes = 128
    nb = s_ref.shape[0]
    lo = jnp.maximum(lo_ref[i], i - (nb - 1))
    mid = jnp.clip(full_ref[i], lo, i)
    q = q_ref[...]
    qpos = i * bq + lax.broadcasted_iota(jnp.int32, (bq, 1), 0)
    qs = jnp.zeros((bq, 1), jnp.int32)
    for c in range(N_DOCS - 1):
        qs = jnp.where(qpos >= bnd_ref[c], bnd_ref[c], qs)

    def raw(kb):
        start = pl.multiple_of(kb * bk, bk)
        s = jnp.dot(q, kt_ref[:, pl.ds(start, bk)], preferred_element_type=jnp.float32)
        return s * scale, start

    def masked(kb):
        s, start = raw(kb)
        kpos = start + lax.broadcasted_iota(jnp.int32, (1, bk), 1)
        ok = (kpos >= qs) & (kpos <= qpos)
        return jnp.where(ok, s, jnp.float32(-1e30)), start

    def keep(kb, m, s):
        s_ref[kb - lo] = s
        for c in range(bk // lanes):
            m = jnp.maximum(m, s[:, c * lanes : (c + 1) * lanes])
        return m

    m = jnp.full((bq, lanes), -1e30, jnp.float32)
    m = lax.fori_loop(lo, mid, lambda kb, m: keep(kb, m, masked(kb)[0]), m)
    m = lax.fori_loop(mid, i, lambda kb, m: keep(kb, m, raw(kb)[0]), m)
    m = keep(i, m, masked(i)[0])
    top = jnp.max(m, axis=1, keepdims=True)

    def accum(kb, carry):
        tot, acc = carry
        p = jnp.exp(s_ref[kb - lo] - top)
        for c in range(bk // lanes):
            tot = tot + p[:, c * lanes : (c + 1) * lanes]
        v = v_ref[pl.ds(pl.multiple_of(kb * bk, bk), bk), :]
        acc = acc + jnp.dot(p.astype(jnp.bfloat16), v, preferred_element_type=jnp.float32)
        return tot, acc

    carry = (jnp.zeros((bq, lanes), jnp.float32), jnp.zeros((bq, q.shape[1]), jnp.float32))
    tot, acc = lax.fori_loop(lo, i + 1, accum, carry)
    total = jnp.sum(tot, axis=1, keepdims=True)
    o_ref[...] = (acc / total).astype(o_ref.dtype)


def attend(queries, key_rows, value_rows, segments):
    length, dim = key_rows.shape
    bq = min(512, length)
    bk = min(512, length)
    n_q = length // bq
    bounds = jnp.sum(
        segments[None, :] < jnp.arange(1, N_DOCS, dtype=jnp.int32)[:, None], axis=1
    ).astype(jnp.int32)

    def doc_start_at(t):
        first = jnp.zeros_like(t)
        for c in range(N_DOCS - 1):
            first = jnp.where(t >= bounds[c], bounds[c], first)
        return first

    firsts = jnp.arange(n_q, dtype=jnp.int32) * bq
    lo_blk = doc_start_at(firsts) // bk
    full_blk = (doc_start_at(firsts + bq - 1) + bk - 1) // bk
    q_rows = queries.reshape(length, dim)
    kernel = functools.partial(_attn_kernel, bq=bq, bk=bk, scale=dim ** (-0.5))
    band = (MAX_DOC + bq - 1) // bk + 1
    out = pl.pallas_call(
        kernel,
        out_shape=jax.ShapeDtypeStruct((length, dim), jnp.bfloat16),
        grid_spec=pltpu.PrefetchScalarGridSpec(
            num_scalar_prefetch=3,
            grid=(n_q,),
            in_specs=[
                pl.BlockSpec((bq, dim), lambda i, lo, full, bnd: (i, 0)),
                pl.BlockSpec((dim, length), lambda i, lo, full, bnd: (0, 0)),
                pl.BlockSpec((length, dim), lambda i, lo, full, bnd: (0, 0)),
            ],
            out_specs=pl.BlockSpec((bq, dim), lambda i, lo, full, bnd: (i, 0)),
            scratch_shapes=[pltpu.VMEM((min(band, n_q), bq, bk), jnp.float32)],
        ),
        compiler_params=pltpu.CompilerParams(vmem_limit_bytes=48 * 1024 * 1024),
        cost_estimate=pl.CostEstimate(
            flops=6 * length * MAX_DOC * dim,
            transcendentals=length * MAX_DOC,
            bytes_accessed=8 * length * dim,
        ),
    )(lo_blk, full_blk, bounds, q_rows, key_rows.T, value_rows)
    return out


def local(queries, keys, values, segment_ids, route_ids, adapter_down, adapter_up):
    n_seq = lax.axis_size("seq")
    n_store = lax.axis_size("store")
    tok_rows = queries.shape[1]
    width = queries.shape[2]
    length = tok_rows * n_seq
    heads_here = HEADS // n_seq
    feat = heads_here * HEAD_DIM
    group = HEADS // KV_HEADS
    devices = n_seq * n_store
    capacity = max(2, 2 * tok_rows // devices)
    slots = n_seq * capacity

    half = tok_rows // 2
    q_send = queries[0].reshape(tok_rows, n_seq, feat)
    paired = jnp.concatenate(
        [keys[0].reshape(tok_rows, KV_HEADS, HEAD_DIM), values[0].reshape(tok_rows, KV_HEADS, HEAD_DIM)],
        axis=2,
    )
    halves = jnp.transpose(paired.reshape(2, half, KV_HEADS, 2 * HEAD_DIM), (0, 2, 1, 3)).reshape(
        2 * KV_HEADS, half, 2 * HEAD_DIM
    )
    dest = jnp.arange(n_seq, dtype=jnp.int32)
    kv_send = jnp.take(halves, (dest % 2) * KV_HEADS + (dest * heads_here) // group, axis=0)
    kv_send = jnp.transpose(kv_send.reshape(n_seq, tok_rows, HEAD_DIM), (1, 0, 2))
    chosen = route_ids[0]
    owners = chosen // EXP_DEV
    one_hot = (owners[:, None] == jnp.arange(devices, dtype=jnp.int32)[None, :]).astype(jnp.int32)
    rank = jnp.sum(jnp.cumsum(one_hot, axis=0) * one_hot, axis=1) - 1
    code = owners * capacity + rank
    meta = jnp.concatenate([segment_ids[0], code, chosen % EXP_DEV]).astype(jnp.bfloat16)
    meta_w = feat + HEAD_DIM
    meta_rows = -(-meta.shape[0] // meta_w)
    meta = jnp.pad(meta, (0, meta_rows * meta_w - meta.shape[0])).reshape(meta_rows, meta_w)
    payload = jnp.concatenate(
        [
            jnp.concatenate([q_send, kv_send], axis=2),
            jnp.broadcast_to(meta[:, None, :], (meta_rows, n_seq, meta_w)),
        ],
        axis=0,
    )
    got_in = lax.all_to_all(payload, "seq", split_axis=1, concat_axis=0, tiled=True)
    got_in = got_in.reshape(n_seq, tok_rows + meta_rows, meta_w)
    q_all = got_in[:, :tok_rows, :feat].reshape(length, heads_here, HEAD_DIM)
    kv_mine = got_in[:, :tok_rows, feat:].reshape(n_seq, half, 2 * HEAD_DIM)
    kv_other = lax.ppermute(kv_mine, "seq", [(i, i ^ 1) for i in range(n_seq)])
    even = lax.axis_index("seq") % 2 == 0
    kv_all = lax.cond(
        even,
        lambda a, b: jnp.stack([a, b], axis=1),
        lambda a, b: jnp.stack([b, a], axis=1),
        kv_mine,
        kv_other,
    ).reshape(length, 2 * HEAD_DIM)
    k_all = kv_all[:, :HEAD_DIM]
    v_all = kv_all[:, HEAD_DIM:]
    meta_all = got_in[:, tok_rows:, :].reshape(n_seq, meta_rows * meta_w)[:, : 3 * tok_rows]
    meta_all = meta_all.astype(jnp.int32)
    segments = meta_all[:, :tok_rows].reshape(length)
    code_all = meta_all[:, tok_rows : 2 * tok_rows]
    adapter_all = meta_all[:, 2 * tok_rows :]

    context = attend(q_all, k_all, v_all, segments).reshape(length, feat)

    pick = code_all[:, None, :] == jnp.arange(devices * capacity, dtype=jnp.int32)[None, :, None]
    pick = pick.astype(jnp.bfloat16)
    send = jnp.einsum(
        "jmt,jtf->mjf",
        pick,
        context.reshape(n_seq, tok_rows, feat),
        preferred_element_type=jnp.float32,
    ).astype(jnp.bfloat16)
    send = send.reshape(devices, slots, feat)
    tags = jnp.einsum(
        "jmt,jt->mj",
        pick,
        (adapter_all.reshape(n_seq, tok_rows) + 1).astype(jnp.bfloat16),
        preferred_element_type=jnp.float32,
    ).reshape(devices, slots) - 1.0
    tag_row = jnp.pad(tags.astype(jnp.bfloat16), ((0, 0), (0, feat - slots)))
    send = jnp.concatenate([send, tag_row[:, None, :]], axis=1)
    got = lax.all_to_all(send, ("seq", "store"), split_axis=0, concat_axis=0, tiled=True)
    got = got.reshape(n_seq, n_store, slots + 1, feat)
    rows = jnp.transpose(
        got[:, :, :slots, :].reshape(n_seq, n_store, capacity, n_seq, feat), (3, 1, 2, 0, 4)
    ).reshape(n_store * slots, width)
    row_tags = jnp.transpose(
        got[0, :, slots, :slots].reshape(n_store, capacity, n_seq), (2, 0, 1)
    ).reshape(n_store * slots, 1).astype(jnp.float32)

    low = jnp.dot(rows, adapter_down, preferred_element_type=jnp.float32)
    lane_owner = (jnp.arange(low.shape[1], dtype=jnp.int32) // RANK).astype(jnp.float32)
    low = jnp.where(row_tags == lane_owner[None, :], low, 0.0).astype(jnp.bfloat16)
    delta = jnp.dot(low, adapter_up, preferred_element_type=jnp.float32).astype(jnp.bfloat16)
    mixed_rows = (rows.astype(jnp.float32) + delta.astype(jnp.float32)).astype(jnp.bfloat16)
    ret = mixed_rows.reshape(devices, capacity, width)
    back = lax.all_to_all(ret, ("seq", "store"), split_axis=0, concat_axis=0, tiled=True)
    mixed = back[owners, rank]
    return mixed[None]


def solution(mesh):
    return jax.shard_map(
        local,
        mesh=mesh,
        in_specs=(
            P("store", "seq", None),
            P("store", "seq", None),
            P("store", "seq", None),
            P("store", "seq"),
            P("store", "seq"),
            P(None, ("seq", "store")),
            P(("seq", "store"), None),
        ),
        out_specs=P("store", "seq", None),
        check_vma=False,
    )
```
